256 devices in a mesh: slab: 64 (over z_hi, x, y), rep: 4 (over z_lo, core).
Axes of the slice: x: 4, y: 4, z: 8 (z_hi: 4, z_lo: 2; z = z_hi * 2 + z_lo), core: 2. Of those that a mesh axis runs over, the one named last changes fastest.
Arguments:
- volume: float32 [2048, 128, 1024], P('slab', 'rep'), may hold values from -6 to 6
- slices_x: bfloat16 [2048, 128, 128], P('slab', 'rep'), may hold values from -6 to 6
- slices_y: bfloat16 [2048, 16, 1024], P('slab'), may hold values from -6 to 6
- slices_z: bfloat16 [256, 128, 1024], P('slab', 'rep'), may hold values from -6 to 6
- profiles: float32 [4, 16, 128], replicated, may hold values from -1 to 2
- profile_index: int32 [25], replicated, may hold values from 0 to 3
- block_shift: int32 [25], replicated, may hold values from 0 to 7
Outputs:
- updated: float32 [2048, 128, 1024], P('slab', 'rep')
The draws below stay inside these ranges and needn't reach their ends.
All inputs are finite; a program needn't handle non-finite values.
Results may differ from the reference program's by a relative error of at most 0.0044.
Values may be sent and summed in bfloat16 or wider, within the bound.
No kernel may reach another device: no remote copies, remote signals or barrier semaphores. Data moves between devices by JAX's collectives and lax.ppermute only.
A program may use at most 64 MiB of HBM per device.

```python
import math
import jax
import jax.numpy as jnp
from jax import lax

BLOCK = 128
SLICES = 16
KPROF = 4
NX = 1024
NZ = 2048
NY = 128
NBLK = 25


def draw_profiles(key, part):
    first, second = jax.random.split(key)
    spacing = BLOCK / SLICES
    spread = 0.75 * spacing
    place = jnp.arange(BLOCK, dtype=jnp.float32)[None, None, :]
    center = (jnp.arange(SLICES, dtype=jnp.float32)[None, :, None] + 0.5) * spacing - 0.5
    envelope = jnp.exp(-0.5 * ((place - center) / spread) ** 2)
    lower, upper, noise = (0.6, 1.4, 0.3)
    factor = jax.random.uniform(first, (KPROF, SLICES, BLOCK), jnp.float32, lower, upper)
    ripple = jax.random.uniform(second, (KPROF, SLICES, BLOCK), jnp.float32, -1.0, 1.0)
    return (envelope * factor + noise * ripple) / math.sqrt(math.sqrt(math.pi) * spread)


def plant(values, own_key, low, high):
    spot = [jax.random.randint(jax.random.fold_in(own_key, axis), (), 0, length) for axis, length in enumerate(values.shape)]
    main_axis = values.shape.index(max(values.shape))
    neighbour = spot[:main_axis] + [(spot[main_axis] + 1) % values.shape[main_axis]] + spot[main_axis + 1:]
    return values.at[tuple(spot)].set(low).at[tuple(neighbour)].set(high)


def level_of(key, extent, shards, low, largest):
    gain, own = 1.0, jax.random.fold_in(key, 6)
    for axis_at, shards_of in shards:
        heights = jnp.exp(jax.random.uniform(jax.random.fold_in(own, axis_at), (shards_of,), jnp.float32, low / len(shards), largest / len(shards)))
        gain = gain * jnp.repeat(heights, extent[axis_at] // shards_of).reshape([-1 if axis == axis_at else 1 for axis in range(len(extent))])
    return gain


def normal_values(stream_key, dims, scale, bound, pieces=(), kind=jnp.bfloat16):
    loudness = level_of(stream_key, dims, pieces, -0.22, 0.18) if pieces else 1.0
    result = jax.random.normal(stream_key, dims, jnp.float32) * scale * loudness
    return jnp.minimum(jnp.maximum(result, -bound), bound).astype(kind)


def setup_inputs(seed: int = 0) -> dict:
    arg_keys = jax.random.split(jax.random.key(seed), 8)
    volume = normal_values(arg_keys[0], (NZ, NY, NX), 1.0, 6.0, ((0, 64), (1, 4)), jnp.float32)
    slices_x = normal_values(arg_keys[1], (NZ, NY, NX // BLOCK * SLICES), 1.0, 6.0, ((0, 64), (1, 4)))
    slices_y = normal_values(arg_keys[2], (NZ, NY // BLOCK * SLICES, NX), 1.0, 6.0, ((0, 64),))
    slices_z = normal_values(arg_keys[3], (NZ // BLOCK * SLICES, NY, NX), 1.0, 6.0, ((0, 64), (1, 4)))
    profiles = draw_profiles(jax.random.fold_in(arg_keys[7], 71), 0)
    profile_index = plant(jax.random.randint(arg_keys[5], (NBLK,), 0, KPROF), jax.random.fold_in(arg_keys[5], 1), 0, KPROF - 1).astype(jnp.int32)
    block_shift = plant(jax.random.randint(arg_keys[6], (NBLK,), 0, BLOCK // SLICES), jax.random.fold_in(arg_keys[6], 1), 0, (BLOCK // SLICES) - 1).astype(jnp.int32)
    return {"volume": volume, "slices_x": slices_x, "slices_y": slices_y, "slices_z": slices_z, "profiles": profiles, "profile_index": profile_index, "block_shift": block_shift}


step_size = 0.5


def profile_blocks(profiles, profile_index, block_shift):
    picked = profiles[profile_index.astype(jnp.int32)]
    columns = jnp.arange(BLOCK, dtype=jnp.int32)
    source = ((columns[None, :] - block_shift[:, None]) % BLOCK).astype(jnp.int32)
    shifted = jnp.take_along_axis(picked, source[:, None, :], axis=2)
    return lax.optimization_barrier(shifted.astype(jnp.bfloat16)).astype(jnp.float32)


def rounded(values):
    return lax.optimization_barrier(values.astype(jnp.bfloat16)).astype(jnp.float32)


def reference(volume, slices_x, slices_y, slices_z, profiles, profile_index, block_shift):
    count_x = NX // BLOCK
    count_y = NY // BLOCK
    count_z = NZ // BLOCK
    mats = profile_blocks(profiles, profile_index, block_shift)
    along_x = mats[:count_x]
    along_y = mats[count_x:count_x + count_y]
    along_z = mats[count_x + count_y:]
    coarse = rounded(volume)

    fwd_x = jnp.einsum('zybl,bsl->zybs', coarse.reshape(NZ, NY, count_x, BLOCK), along_x).reshape(NZ, NY, count_x * SLICES)
    resid_x = rounded(slices_x.astype(jnp.float32) - fwd_x)
    corr = jnp.einsum('zybs,bsl->zybl', resid_x.reshape(NZ, NY, count_x, SLICES), along_x).reshape(NZ, NY, NX)

    fwd_y = jnp.einsum('zblx,bsl->zbsx', coarse.reshape(NZ, count_y, BLOCK, NX), along_y).reshape(NZ, count_y * SLICES, NX)
    resid_y = rounded(slices_y.astype(jnp.float32) - fwd_y)
    corr = corr + jnp.einsum('zbsx,bsl->zblx', resid_y.reshape(NZ, count_y, SLICES, NX), along_y).reshape(NZ, NY, NX)

    fwd_z = jnp.einsum('blyx,bsl->bsyx', coarse.reshape(count_z, BLOCK, NY, NX), along_z).reshape(count_z * SLICES, NY, NX)
    resid_z = rounded(slices_z.astype(jnp.float32) - fwd_z)
    corr = corr + jnp.einsum('bsyx,bsl->blyx', resid_z.reshape(count_z, SLICES, NY, NX), along_z).reshape(NZ, NY, NX)

    return volume + step_size * corr
```

```python
import jax
import jax.numpy as jnp
from jax import lax
from jax.sharding import Mesh, PartitionSpec as P

BLOCK = 128
SLICES = 16


step_size = 0.5


def block_mats(profiles, profile_index, block_shift):
    kinds = profiles.shape[0]
    span = profiles.shape[2]
    onehot = (profile_index[:, None] == jnp.arange(kinds, dtype=jnp.int32)[None, :]).astype(
        jnp.float32
    )
    picked = jnp.einsum("bk,ksl->bsl", onehot, profiles, precision=lax.Precision.HIGHEST)
    columns = jnp.arange(span, dtype=jnp.int32)
    target = (columns[None, :] + block_shift[:, None]) % span
    moving = (target[:, :, None] == columns[None, None, :]).astype(jnp.float32)
    shifted = jnp.einsum("bsj,bjl->bsl", picked, moving, precision=lax.Precision.HIGHEST)
    return shifted.astype(jnp.bfloat16)


def banded_matrix(along):
    count = along.shape[0]
    identity = jnp.eye(count, dtype=jnp.bfloat16)
    return (along[:, :, None, :] * identity[:, None, :, None]).reshape(
        count * SLICES, count * BLOCK
    )


def shards(volume, slices_x, slices_y, slices_z, profiles, profile_index, block_shift):
    planes, rows_here, width = volume.shape
    count_x = width // BLOCK
    count_y = slices_y.shape[1] // SLICES
    mats = block_mats(profiles, profile_index, block_shift)
    along_x = mats[:count_x]
    along_y = mats[count_x : count_x + count_y]
    along_z = mats[count_x + count_y :]
    coarse = volume.astype(jnp.bfloat16)

    banded_x = banded_matrix(along_x)
    flat_coarse = coarse.reshape(planes * rows_here, width)
    fwd_x = lax.dot_general(
        flat_coarse, banded_x, (((1,), (1,)), ((), ())), preferred_element_type=jnp.float32
    )
    resid_x = (
        slices_x.reshape(planes * rows_here, count_x * SLICES).astype(jnp.float32) - fwd_x
    ).astype(jnp.bfloat16)
    corr_x = jnp.dot(resid_x, banded_x, preferred_element_type=jnp.float32).reshape(
        planes, rows_here, width
    )

    rep = lax.axis_index("rep")
    nrep = lax.axis_size("rep")
    band_y = lax.dynamic_slice_in_dim(along_y[0], rep * rows_here, rows_here, 1)
    partial_y = jnp.einsum("sl,zlx->zsx", band_y, coarse, preferred_element_type=jnp.float32)
    fwd_y = lax.psum_scatter(partial_y, "rep", scatter_dimension=0, tiled=True)
    part_z = planes // nrep
    obs_y = lax.dynamic_slice_in_dim(slices_y, rep * part_z, part_z, 0)
    resid_y = (obs_y.astype(jnp.float32) - fwd_y).astype(jnp.bfloat16)
    resid_y = lax.all_gather(resid_y, "rep", axis=0, tiled=True)
    corr_y = jnp.einsum("sl,zsx->zlx", band_y, resid_y, preferred_element_type=jnp.float32)

    zb = lax.axis_index("zb")
    zq = lax.axis_index("zq")
    mat_z = lax.dynamic_index_in_dim(along_z, zb, 0, keepdims=False)
    band_z = lax.dynamic_slice_in_dim(mat_z, zq * planes, planes, 1)
    partial_z = jnp.einsum("sl,lyx->syx", band_z, coarse, preferred_element_type=jnp.float32)
    fwd_z = lax.psum_scatter(partial_z, "zq", scatter_dimension=0, tiled=True)
    resid_z = (slices_z.astype(jnp.float32) - fwd_z).astype(jnp.bfloat16)
    resid_z = lax.all_gather(resid_z, "zq", axis=0, tiled=True)
    corr_z = jnp.einsum("sl,syx->lyx", band_z, resid_z, preferred_element_type=jnp.float32)

    return volume + step_size * (corr_x + corr_y + corr_z)


def solution(mesh):
    nslab, nrep = mesh.devices.shape
    slab = ("zb", "zq")

    def run(volume, *rest):
        group = BLOCK // (volume.shape[0] // nslab)
        inner = Mesh(mesh.devices.reshape(nslab // group, group, nrep), ("zb", "zq", "rep"))
        return jax.shard_map(
            shards,
            mesh=inner,
            in_specs=(
                P(slab, "rep", None),
                P(slab, "rep", None),
                P(slab, None, None),
                P(slab, "rep", None),
                P(),
                P(),
                P(),
            ),
            out_specs=P(slab, "rep", None),
            check_vma=False,
        )(volume, *rest)

    return run
```

```python
import jax
import jax.numpy as jnp
from jax import lax
from jax.sharding import Mesh, PartitionSpec as P

BLOCK = 128
SLICES = 16


step_size = 0.5


def block_mats(profiles, profile_index, block_shift):
    kinds = profiles.shape[0]
    span = profiles.shape[2]
    onehot = (profile_index[:, None] == jnp.arange(kinds, dtype=jnp.int32)[None, :]).astype(
        jnp.float32
    )
    picked = jnp.einsum("bk,ksl->bsl", onehot, profiles, precision=lax.Precision.HIGHEST)
    columns = jnp.arange(span, dtype=jnp.int32)
    target = (columns[None, :] + block_shift[:, None]) % span
    moving = (target[:, :, None] == columns[None, None, :]).astype(jnp.float32)
    shifted = jnp.einsum("bsj,bjl->bsl", picked, moving, precision=lax.Precision.HIGHEST)
    return shifted.astype(jnp.bfloat16)


def banded_matrix(along):
    count = along.shape[0]
    identity = jnp.eye(count, dtype=jnp.bfloat16)
    return (along[:, :, None, :] * identity[:, None, :, None]).reshape(
        count * SLICES, count * BLOCK
    )


def halve(values, axis, me):
    half = values.shape[0] // 2
    keep = lax.dynamic_slice_in_dim(values, me * half, half, 0)
    give = lax.dynamic_slice_in_dim(values, (1 - me) * half, half, 0)
    return keep + lax.ppermute(give, axis, [(0, 1), (1, 0)])


def double(values, axis, me):
    other = lax.ppermute(values, axis, [(0, 1), (1, 0)])
    low = jnp.where(me == 0, values, other)
    high = jnp.where(me == 0, other, values)
    return jnp.concatenate([low, high], 0)


def shards(volume, slices_x, slices_y, slices_z, profiles, profile_index, block_shift):
    planes, rows_here, width = volume.shape
    count_x = width // BLOCK
    count_y = slices_y.shape[1] // SLICES
    mats = block_mats(profiles, profile_index, block_shift)
    along_x = mats[:count_x]
    along_y = mats[count_x : count_x + count_y]
    along_z = mats[count_x + count_y :]
    coarse = volume.astype(jnp.bfloat16)

    banded_x = banded_matrix(along_x)
    flat_coarse = coarse.reshape(planes * rows_here, width)
    fwd_x = lax.dot_general(
        flat_coarse, banded_x, (((1,), (1,)), ((), ())), preferred_element_type=jnp.float32
    )
    resid_x = (
        slices_x.reshape(planes * rows_here, count_x * SLICES).astype(jnp.float32) - fwd_x
    ).astype(jnp.bfloat16)
    corr_x = jnp.dot(resid_x, banded_x, preferred_element_type=jnp.float32).reshape(
        planes, rows_here, width
    )

    zl = lax.axis_index("zl")
    co = lax.axis_index("co")
    rep = zl * 2 + co
    band_y = lax.dynamic_slice_in_dim(along_y[0], rep * rows_here, rows_here, 1)
    partial_y = jnp.einsum("sl,zlx->zsx", band_y, coarse, preferred_element_type=jnp.float32)
    fwd_y = halve(partial_y, "co", co)
    fwd_y = halve(fwd_y, "zl", zl)
    part_z = planes // 4
    obs_y = lax.dynamic_slice_in_dim(slices_y, (co * 2 + zl) * part_z, part_z, 0)
    resid_y = (obs_y.astype(jnp.float32) - fwd_y).astype(jnp.bfloat16)
    resid_y = double(resid_y, "zl", zl)
    resid_y = double(resid_y, "co", co)
    corr_y = jnp.einsum("sl,zsx->zlx", band_y, resid_y, preferred_element_type=jnp.float32)

    zb = lax.axis_index("zb")
    zq = lax.axis_index("zq")
    group = lax.axis_size("zq")
    mat_z = lax.dynamic_index_in_dim(along_z, zb, 0, keepdims=False)
    band_z = lax.dynamic_slice_in_dim(mat_z, zq * planes, planes, 1)
    partial_z = jnp.einsum("sl,lyx->syx", band_z, coarse, preferred_element_type=jnp.float32)
    piece = SLICES // group
    fwd_z = lax.dynamic_slice_in_dim(partial_z, zq * piece, piece, 0)
    for k in range(1, group):
        dest = (zq + k) % group
        sent = lax.dynamic_slice_in_dim(partial_z, dest * piece, piece, 0)
        fwd_z = fwd_z + lax.ppermute(sent, "zq", [(j, (j + k) % group) for j in range(group)])
    resid_z = (slices_z.astype(jnp.float32) - fwd_z).astype(jnp.bfloat16)
    pieces = [resid_z]
    rows = [lax.dynamic_slice_in_dim(band_z, zq * piece, piece, 0)]
    for k in range(1, group):
        pieces.append(lax.ppermute(resid_z, "zq", [(j, (j + k) % group) for j in range(group)]))
        src = (zq - k + group) % group
        rows.append(lax.dynamic_slice_in_dim(band_z, src * piece, piece, 0))
    corr_z = jnp.einsum(
        "sl,syx->lyx",
        jnp.concatenate(rows, 0),
        jnp.concatenate(pieces, 0),
        preferred_element_type=jnp.float32,
    )

    return volume + step_size * (corr_x + corr_y + corr_z)


def solution(mesh):
    nslab, nrep = mesh.devices.shape
    slab = ("zb", "zq")
    rep = ("zl", "co")

    def run(volume, *rest):
        group = BLOCK // (volume.shape[0] // nslab)
        inner = Mesh(
            mesh.devices.reshape(nslab // group, group, 2, nrep // 2), ("zb", "zq", "zl", "co")
        )
        return jax.shard_map(
            shards,
            mesh=inner,
            in_specs=(
                P(slab, rep, None),
                P(slab, rep, None),
                P(slab, None, None),
                P(slab, rep, None),
                P(),
                P(),
                P(),
            ),
            out_specs=P(slab, rep, None),
            check_vma=False,
        )(volume, *rest)

    return run
```

```python
import jax
import jax.numpy as jnp
from jax import lax
from jax.sharding import Mesh, PartitionSpec as P

BLOCK = 128
SLICES = 16


step_size = 0.5


def block_mats(profiles, profile_index, block_shift):
    kinds = profiles.shape[0]
    span = profiles.shape[2]
    onehot = (profile_index[:, None] == jnp.arange(kinds, dtype=jnp.int32)[None, :]).astype(
        jnp.float32
    )
    picked = jnp.einsum("bk,ksl->bsl", onehot, profiles, precision=lax.Precision.HIGHEST)
    columns = jnp.arange(span, dtype=jnp.int32)
    target = (columns[None, :] + block_shift[:, None]) % span
    moving = (target[:, :, None] == columns[None, None, :]).astype(jnp.float32)
    shifted = jnp.einsum("bsj,bjl->bsl", picked, moving, precision=lax.Precision.HIGHEST)
    return shifted.astype(jnp.bfloat16)


def banded_matrix(along):
    count = along.shape[0]
    identity = jnp.eye(count, dtype=jnp.bfloat16)
    return (along[:, :, None, :] * identity[:, None, :, None]).reshape(
        count * SLICES, count * BLOCK
    )


def halve(values, axis, me):
    half = values.shape[0] // 2
    keep = lax.dynamic_slice_in_dim(values, me * half, half, 0)
    give = lax.dynamic_slice_in_dim(values, (1 - me) * half, half, 0)
    got = lax.ppermute(give.astype(jnp.bfloat16), axis, [(0, 1), (1, 0)])
    return keep + got.astype(jnp.float32)


def double(values, axis, me):
    other = lax.ppermute(values, axis, [(0, 1), (1, 0)])
    low = jnp.where(me == 0, values, other)
    high = jnp.where(me == 0, other, values)
    return jnp.concatenate([low, high], 0)


def shards(volume, slices_x, slices_y, slices_z, profiles, profile_index, block_shift):
    planes, rows_here, width = volume.shape
    count_x = width // BLOCK
    count_y = slices_y.shape[1] // SLICES
    mats = block_mats(profiles, profile_index, block_shift)
    along_x = mats[:count_x]
    along_y = mats[count_x : count_x + count_y]
    along_z = mats[count_x + count_y :]
    coarse = volume.astype(jnp.bfloat16)

    banded_x = banded_matrix(along_x)
    flat_coarse = coarse.reshape(planes * rows_here, width)
    fwd_x = lax.dot_general(
        flat_coarse, banded_x, (((1,), (1,)), ((), ())), preferred_element_type=jnp.float32
    )
    resid_x = (
        slices_x.reshape(planes * rows_here, count_x * SLICES).astype(jnp.float32) - fwd_x
    ).astype(jnp.bfloat16)
    corr_x = jnp.dot(resid_x, banded_x, preferred_element_type=jnp.float32).reshape(
        planes, rows_here, width
    )

    zl = lax.axis_index("zl")
    co = lax.axis_index("co")
    rep = zl * 2 + co
    band_y = lax.dynamic_slice_in_dim(along_y[0], rep * rows_here, rows_here, 1)
    partial_y = jnp.einsum("sl,zlx->zsx", band_y, coarse, preferred_element_type=jnp.float32)
    fwd_y = halve(partial_y, "co", co)
    fwd_y = halve(fwd_y, "zl", zl)
    part_z = planes // 4
    obs_y = lax.dynamic_slice_in_dim(slices_y, (co * 2 + zl) * part_z, part_z, 0)
    resid_y = (obs_y.astype(jnp.float32) - fwd_y).astype(jnp.bfloat16)
    resid_y = double(resid_y, "zl", zl)
    resid_y = double(resid_y, "co", co)
    corr_y = jnp.einsum("sl,zsx->zlx", band_y, resid_y, preferred_element_type=jnp.float32)

    zb = lax.axis_index("zb")
    zq = lax.axis_index("zq")
    group = lax.axis_size("zq")
    mat_z = lax.dynamic_index_in_dim(along_z, zb, 0, keepdims=False)
    band_z = lax.dynamic_slice_in_dim(mat_z, zq * planes, planes, 1)
    partial_z = jnp.einsum("sl,lyx->syx", band_z, coarse, preferred_element_type=jnp.float32)
    piece = SLICES // group
    fwd_z = lax.dynamic_slice_in_dim(partial_z, zq * piece, piece, 0)
    for k in range(1, group):
        dest = (zq + k) % group
        sent = lax.dynamic_slice_in_dim(partial_z, dest * piece, piece, 0).astype(jnp.bfloat16)
        got = lax.ppermute(sent, "zq", [(j, (j + k) % group) for j in range(group)])
        fwd_z = fwd_z + got.astype(jnp.float32)
    resid_z = (slices_z.astype(jnp.float32) - fwd_z).astype(jnp.bfloat16)
    pieces = [resid_z]
    rows = [lax.dynamic_slice_in_dim(band_z, zq * piece, piece, 0)]
    for k in range(1, group):
        pieces.append(lax.ppermute(resid_z, "zq", [(j, (j + k) % group) for j in range(group)]))
        src = (zq - k + group) % group
        rows.append(lax.dynamic_slice_in_dim(band_z, src * piece, piece, 0))
    corr_z = jnp.einsum(
        "sl,syx->lyx",
        jnp.concatenate(rows, 0),
        jnp.concatenate(pieces, 0),
        preferred_element_type=jnp.float32,
    )

    return volume + step_size * (corr_x + corr_y + corr_z)


def solution(mesh):
    nslab, nrep = mesh.devices.shape
    slab = ("zb", "zq")
    rep = ("zl", "co")

    def run(volume, *rest):
        group = BLOCK // (volume.shape[0] // nslab)
        inner = Mesh(
            mesh.devices.reshape(nslab // group, group, 2, nrep // 2), ("zb", "zq", "zl", "co")
        )
        return jax.shard_map(
            shards,
            mesh=inner,
            in_specs=(
                P(slab, rep, None),
                P(slab, rep, None),
                P(slab, None, None),
                P(slab, rep, None),
                P(),
                P(),
                P(),
            ),
            out_specs=P(slab, rep, None),
            check_vma=False,
        )(volume, *rest)

    return run
```

```python
import jax
import jax.numpy as jnp
from jax import lax
from jax.sharding import Mesh, PartitionSpec as P

BLOCK = 128
SLICES = 16


step_size = 0.5


def block_mats(profiles, profile_index, block_shift):
    kinds = profiles.shape[0]
    span = profiles.shape[2]
    onehot = (profile_index[:, None] == jnp.arange(kinds, dtype=jnp.int32)[None, :]).astype(
        jnp.float32
    )
    picked = jnp.einsum("bk,ksl->bsl", onehot, profiles, precision=lax.Precision.HIGHEST)
    columns = jnp.arange(span, dtype=jnp.int32)
    target = (columns[None, :] + block_shift[:, None]) % span
    moving = (target[:, :, None] == columns[None, None, :]).astype(jnp.float32)
    shifted = jnp.einsum("bsj,bjl->bsl", picked, moving, precision=lax.Precision.HIGHEST)
    return shifted.astype(jnp.bfloat16)


def banded_matrix(along):
    count = along.shape[0]
    identity = jnp.eye(count, dtype=jnp.bfloat16)
    return (along[:, :, None, :] * identity[:, None, :, None]).reshape(
        count * SLICES, count * BLOCK
    )


RING = 4
PLUS = [(j, (j + 1) % RING) for j in range(RING)]
MINUS = [(j, (j - 1) % RING) for j in range(RING)]


def ring_send(values, pairs):
    return lax.ppermute(values, "zq", pairs)


def ring_reduce(partial, me, piece):
    cut = partial.shape[1] // 2

    def chunk(d):
        return lax.dynamic_slice_in_dim(partial, ((me + d) % RING) * piece, piece, 0)

    def lo(v):
        return v[:, :cut]

    def hi(v):
        return v[:, cut:]

    def wire(v):
        return v.astype(jnp.bfloat16)

    own, nxt, far, prv = chunk(0), chunk(1), chunk(2), chunk(3)
    got_p_far = ring_send(wire(lo(far)), PLUS).astype(jnp.float32)
    got_p_own = ring_send(wire(hi(nxt)), PLUS).astype(jnp.float32)
    got_m_far = ring_send(wire(hi(far)), MINUS).astype(jnp.float32)
    got_m_own = ring_send(wire(lo(prv)), MINUS).astype(jnp.float32)
    got2_p = ring_send(wire(got_p_far + lo(nxt)), PLUS).astype(jnp.float32)
    got2_m = ring_send(wire(got_m_far + hi(prv)), MINUS).astype(jnp.float32)
    low = lo(own) + got_m_own + got2_p
    high = hi(own) + got_p_own + got2_m
    return jnp.concatenate([low, high], 1)


def ring_gather(values):
    cut = values.shape[1] // 2
    from_prev = ring_send(values, PLUS)
    from_next = ring_send(values, MINUS)
    far_lo = ring_send(from_prev[:, :cut], PLUS)
    far_hi = ring_send(from_next[:, cut:], MINUS)
    far = jnp.concatenate([far_lo, far_hi], 1)
    return [values, from_prev, from_next, far], [0, RING - 1, 1, 2]


def halve(values, axis, me):
    half = values.shape[0] // 2
    keep = lax.dynamic_slice_in_dim(values, me * half, half, 0)
    give = lax.dynamic_slice_in_dim(values, (1 - me) * half, half, 0)
    got = lax.ppermute(give.astype(jnp.bfloat16), axis, [(0, 1), (1, 0)])
    return keep + got.astype(jnp.float32)


def double(values, axis, me):
    other = lax.ppermute(values, axis, [(0, 1), (1, 0)])
    low = jnp.where(me == 0, values, other)
    high = jnp.where(me == 0, other, values)
    return jnp.concatenate([low, high], 0)


def shards(volume, slices_x, slices_y, slices_z, profiles, profile_index, block_shift):
    planes, rows_here, width = volume.shape
    count_x = width // BLOCK
    count_y = slices_y.shape[1] // SLICES
    mats = block_mats(profiles, profile_index, block_shift)
    along_x = mats[:count_x]
    along_y = mats[count_x : count_x + count_y]
    along_z = mats[count_x + count_y :]
    coarse = volume.astype(jnp.bfloat16)

    banded_x = banded_matrix(along_x)
    flat_coarse = coarse.reshape(planes * rows_here, width)
    fwd_x = lax.dot_general(
        flat_coarse, banded_x, (((1,), (1,)), ((), ())), preferred_element_type=jnp.float32
    )
    resid_x = (
        slices_x.reshape(planes * rows_here, count_x * SLICES).astype(jnp.float32) - fwd_x
    ).astype(jnp.bfloat16)
    corr_x = jnp.dot(resid_x, banded_x, preferred_element_type=jnp.float32).reshape(
        planes, rows_here, width
    )

    zl = lax.axis_index("zl")
    co = lax.axis_index("co")
    rep = zl * 2 + co
    band_y = lax.dynamic_slice_in_dim(along_y[0], rep * rows_here, rows_here, 1)
    partial_y = jnp.einsum("sl,zlx->zsx", band_y, coarse, preferred_element_type=jnp.float32)
    fwd_y = halve(partial_y, "co", co)
    fwd_y = halve(fwd_y, "zl", zl)
    part_z = planes // 4
    obs_y = lax.dynamic_slice_in_dim(slices_y, (co * 2 + zl) * part_z, part_z, 0)
    resid_y = (obs_y.astype(jnp.float32) - fwd_y).astype(jnp.bfloat16)
    resid_y = double(resid_y, "zl", zl)
    resid_y = double(resid_y, "co", co)
    corr_y = jnp.einsum("sl,zsx->zlx", band_y, resid_y, preferred_element_type=jnp.float32)

    zb = lax.axis_index("zb")
    zq = lax.axis_index("zq")
    group = lax.axis_size("zq")
    mat_z = lax.dynamic_index_in_dim(along_z, zb, 0, keepdims=False)
    band_z = lax.dynamic_slice_in_dim(mat_z, zq * planes, planes, 1)
    partial_z = jnp.einsum("sl,lyx->syx", band_z, coarse, preferred_element_type=jnp.float32)
    piece = SLICES // group
    fwd_z = ring_reduce(partial_z, zq, piece)
    resid_z = (slices_z.astype(jnp.float32) - fwd_z).astype(jnp.bfloat16)
    pieces, sources = ring_gather(resid_z)
    rows = [lax.dynamic_slice_in_dim(band_z, ((zq + d) % group) * piece, piece, 0) for d in sources]
    corr_z = jnp.einsum(
        "sl,syx->lyx",
        jnp.concatenate(rows, 0),
        jnp.concatenate(pieces, 0),
        preferred_element_type=jnp.float32,
    )

    return volume + step_size * (corr_x + corr_y + corr_z)


def solution(mesh):
    nslab, nrep = mesh.devices.shape
    slab = ("zb", "zq")
    rep = ("zl", "co")

    def run(volume, *rest):
        group = BLOCK // (volume.shape[0] // nslab)
        inner = Mesh(
            mesh.devices.reshape(nslab // group, group, 2, nrep // 2), ("zb", "zq", "zl", "co")
        )
        return jax.shard_map(
            shards,
            mesh=inner,
            in_specs=(
                P(slab, rep, None),
                P(slab, rep, None),
                P(slab, None, None),
                P(slab, rep, None),
                P(),
                P(),
                P(),
            ),
            out_specs=P(slab, rep, None),
            check_vma=False,
        )(volume, *rest)

    return run
```

```python
import jax
import jax.numpy as jnp
from jax import lax
from jax.sharding import Mesh, PartitionSpec as P

BLOCK = 128
SLICES = 16


step_size = 0.5


def block_mats(profiles, profile_index, block_shift):
    kinds = profiles.shape[0]
    span = profiles.shape[2]
    onehot = (profile_index[:, None] == jnp.arange(kinds, dtype=jnp.int32)[None, :]).astype(
        jnp.float32
    )
    picked = jnp.einsum("bk,ksl->bsl", onehot, profiles, precision=lax.Precision.HIGHEST)
    columns = jnp.arange(span, dtype=jnp.int32)
    target = (columns[None, :] + block_shift[:, None]) % span
    moving = (target[:, :, None] == columns[None, None, :]).astype(jnp.float32)
    shifted = jnp.einsum("bsj,bjl->bsl", picked, moving, precision=lax.Precision.HIGHEST)
    return shifted.astype(jnp.bfloat16)


def banded_matrix(along):
    count = along.shape[0]
    identity = jnp.eye(count, dtype=jnp.bfloat16)
    return (along[:, :, None, :] * identity[:, None, :, None]).reshape(
        count * SLICES, count * BLOCK
    )


def halve(values, axis, me):
    half = values.shape[0] // 2
    keep = lax.dynamic_slice_in_dim(values, me * half, half, 0)
    give = lax.dynamic_slice_in_dim(values, (1 - me) * half, half, 0)
    got = lax.ppermute(give.astype(jnp.bfloat16), axis, [(0, 1), (1, 0)])
    return keep + got.astype(jnp.float32)


def double(values, axis, me):
    other = lax.ppermute(values, axis, [(0, 1), (1, 0)])
    low = jnp.where(me == 0, values, other)
    high = jnp.where(me == 0, other, values)
    return jnp.concatenate([low, high], 0)


def shards(volume, slices_x, slices_y, slices_z, profiles, profile_index, block_shift):
    planes, rows_here, width = volume.shape
    count_x = width // BLOCK
    count_y = slices_y.shape[1] // SLICES
    mats = block_mats(profiles, profile_index, block_shift)
    along_x = mats[:count_x]
    along_y = mats[count_x : count_x + count_y]
    along_z = mats[count_x + count_y :]
    coarse = volume.astype(jnp.bfloat16)

    banded_x = banded_matrix(along_x)
    flat_coarse = coarse.reshape(planes * rows_here, width)
    fwd_x = lax.dot_general(
        flat_coarse, banded_x, (((1,), (1,)), ((), ())), preferred_element_type=jnp.float32
    )
    resid_x = (
        slices_x.reshape(planes * rows_here, count_x * SLICES).astype(jnp.float32) - fwd_x
    ).astype(jnp.bfloat16)
    corr_x = jnp.dot(resid_x, banded_x, preferred_element_type=jnp.float32).reshape(
        planes, rows_here, width
    )

    zl = lax.axis_index("zl")
    co = lax.axis_index("co")
    rep = zl * 2 + co
    band_y = lax.dynamic_slice_in_dim(along_y[0], rep * rows_here, rows_here, 1)
    half = planes // 2
    keep_y = jnp.einsum(
        "sl,zlx->zsx",
        band_y,
        lax.dynamic_slice_in_dim(coarse, co * half, half, 0),
        preferred_element_type=jnp.float32,
    )
    give_y = jnp.einsum(
        "sl,zlx->zsx",
        band_y,
        lax.dynamic_slice_in_dim(coarse, (1 - co) * half, half, 0),
        preferred_element_type=jnp.float32,
    ).astype(jnp.bfloat16)
    fwd_y = keep_y + lax.ppermute(give_y, "co", [(0, 1), (1, 0)]).astype(jnp.float32)
    fwd_y = halve(fwd_y, "zl", zl)
    part_z = planes // 4
    obs_y = lax.dynamic_slice_in_dim(slices_y, (co * 2 + zl) * part_z, part_z, 0)
    resid_y = (obs_y.astype(jnp.float32) - fwd_y).astype(jnp.bfloat16)
    resid_y = double(resid_y, "zl", zl)
    resid_y = double(resid_y, "co", co)
    corr_y = jnp.einsum("sl,zsx->zlx", band_y, resid_y, preferred_element_type=jnp.float32)

    zb = lax.axis_index("zb")
    zq = lax.axis_index("zq")
    group = lax.axis_size("zq")
    mat_z = lax.dynamic_index_in_dim(along_z, zb, 0, keepdims=False)
    band_z = lax.dynamic_slice_in_dim(mat_z, zq * planes, planes, 1)
    piece = SLICES // group
    own_rows = lax.dynamic_slice_in_dim(band_z, zq * piece, piece, 0)
    fwd_z = jnp.einsum("sl,lyx->syx", own_rows, coarse, preferred_element_type=jnp.float32)
    far_rows = jnp.concatenate(
        [lax.dynamic_slice_in_dim(band_z, ((zq + k) % group) * piece, piece, 0) for k in range(1, group)],
        0,
    )
    far_z = jnp.einsum(
        "sl,lyx->syx", far_rows, coarse, preferred_element_type=jnp.float32
    ).astype(jnp.bfloat16)
    for k in range(1, group):
        sent = far_z[(k - 1) * piece : k * piece]
        got = lax.ppermute(sent, "zq", [(j, (j + k) % group) for j in range(group)])
        fwd_z = fwd_z + got.astype(jnp.float32)
    base, fwd_z = lax.optimization_barrier((volume + step_size * corr_x, fwd_z))
    resid_z = (slices_z.astype(jnp.float32) - fwd_z).astype(jnp.bfloat16)
    pieces = [resid_z]
    rows = [lax.dynamic_slice_in_dim(band_z, zq * piece, piece, 0)]
    for k in range(1, group):
        pieces.append(lax.ppermute(resid_z, "zq", [(j, (j + k) % group) for j in range(group)]))
        src = (zq - k + group) % group
        rows.append(lax.dynamic_slice_in_dim(band_z, src * piece, piece, 0))
    corr_z = jnp.einsum(
        "sl,syx->lyx",
        jnp.concatenate(rows, 0),
        jnp.concatenate(pieces, 0),
        preferred_element_type=jnp.float32,
    )

    return base + step_size * (corr_y + corr_z)


def solution(mesh):
    nslab, nrep = mesh.devices.shape
    slab = ("zb", "zq")
    rep = ("zl", "co")

    def run(volume, *rest):
        group = BLOCK // (volume.shape[0] // nslab)
        inner = Mesh(
            mesh.devices.reshape(nslab // group, group, 2, nrep // 2), ("zb", "zq", "zl", "co")
        )
        return jax.shard_map(
            shards,
            mesh=inner,
            in_specs=(
                P(slab, rep, None),
                P(slab, rep, None),
                P(slab, None, None),
                P(slab, rep, None),
                P(),
                P(),
                P(),
            ),
            out_specs=P(slab, rep, None),
            check_vma=False,
        )(volume, *rest)

    return run
```

```python
import jax
import jax.numpy as jnp
from jax import lax
from jax.sharding import Mesh, PartitionSpec as P

BLOCK = 128
SLICES = 16


step_size = 0.5


def block_mats(profiles, profile_index, block_shift):
    kinds = profiles.shape[0]
    span = profiles.shape[2]
    onehot = (profile_index[:, None] == jnp.arange(kinds, dtype=jnp.int32)[None, :]).astype(
        jnp.float32
    )
    picked = jnp.einsum("bk,ksl->bsl", onehot, profiles, precision=lax.Precision.HIGHEST)
    columns = jnp.arange(span, dtype=jnp.int32)
    target = (columns[None, :] + block_shift[:, None]) % span
    moving = (target[:, :, None] == columns[None, None, :]).astype(jnp.float32)
    shifted = jnp.einsum("bsj,bjl->bsl", picked, moving, precision=lax.Precision.HIGHEST)
    return shifted.astype(jnp.bfloat16)


def banded_matrix(along):
    count = along.shape[0]
    identity = jnp.eye(count, dtype=jnp.bfloat16)
    return (along[:, :, None, :] * identity[:, None, :, None]).reshape(
        count * SLICES, count * BLOCK
    )


def halve(values, axis, me):
    half = values.shape[0] // 2
    keep = lax.dynamic_slice_in_dim(values, me * half, half, 0)
    give = lax.dynamic_slice_in_dim(values, (1 - me) * half, half, 0)
    got = lax.ppermute(give.astype(jnp.bfloat16), axis, [(0, 1), (1, 0)])
    return keep + got.astype(jnp.float32)


def double(values, axis, me):
    other = lax.ppermute(values, axis, [(0, 1), (1, 0)])
    low = jnp.where(me == 0, values, other)
    high = jnp.where(me == 0, other, values)
    return jnp.concatenate([low, high], 0)


def shards(volume, slices_x, slices_y, slices_z, profiles, profile_index, block_shift):
    planes, rows_here, width = volume.shape
    count_x = width // BLOCK
    count_y = slices_y.shape[1] // SLICES
    mats = block_mats(profiles, profile_index, block_shift)
    along_x = mats[:count_x]
    along_y = mats[count_x : count_x + count_y]
    along_z = mats[count_x + count_y :]
    coarse = volume.astype(jnp.bfloat16)

    banded_x = banded_matrix(along_x)
    flat_coarse = coarse.reshape(planes * rows_here, width)
    fwd_x = lax.dot_general(
        flat_coarse, banded_x, (((1,), (1,)), ((), ())), preferred_element_type=jnp.float32
    )
    resid_x = (
        slices_x.reshape(planes * rows_here, count_x * SLICES).astype(jnp.float32) - fwd_x
    ).astype(jnp.bfloat16)
    corr_x = jnp.dot(resid_x, banded_x, preferred_element_type=jnp.float32).reshape(
        planes, rows_here, width
    )

    zl = lax.axis_index("zl")
    co = lax.axis_index("co")
    rep = zl * 2 + co
    band_y = lax.dynamic_slice_in_dim(along_y[0], rep * rows_here, rows_here, 1)
    half = planes // 2
    keep_y = jnp.einsum(
        "sl,zlx->zsx",
        band_y,
        lax.dynamic_slice_in_dim(coarse, co * half, half, 0),
        preferred_element_type=jnp.float32,
    )
    give_y = jnp.einsum(
        "sl,zlx->zsx",
        band_y,
        lax.dynamic_slice_in_dim(coarse, (1 - co) * half, half, 0),
        preferred_element_type=jnp.float32,
    ).astype(jnp.bfloat16)
    fwd_y = keep_y + lax.ppermute(give_y, "co", [(0, 1), (1, 0)]).astype(jnp.float32)
    fwd_y = halve(fwd_y, "zl", zl)
    part_z = planes // 4
    obs_y = lax.dynamic_slice_in_dim(slices_y, (co * 2 + zl) * part_z, part_z, 0)
    resid_y = (obs_y.astype(jnp.float32) - fwd_y).astype(jnp.bfloat16)
    resid_y = double(resid_y, "zl", zl)
    resid_y = double(resid_y, "co", co)
    corr_y = jnp.einsum("sl,zsx->zlx", band_y, resid_y, preferred_element_type=jnp.float32)

    zb = lax.axis_index("zb")
    zq = lax.axis_index("zq")
    group = lax.axis_size("zq")
    mat_z = lax.dynamic_index_in_dim(along_z, zb, 0, keepdims=False)
    band_z = lax.dynamic_slice_in_dim(mat_z, zq * planes, planes, 1)
    piece = SLICES // group
    own_rows = lax.dynamic_slice_in_dim(band_z, zq * piece, piece, 0)
    fwd_z = jnp.einsum("sl,lyx->syx", own_rows, coarse, preferred_element_type=jnp.float32)
    far_rows = jnp.concatenate(
        [lax.dynamic_slice_in_dim(band_z, ((zq + k) % group) * piece, piece, 0) for k in range(1, group)],
        0,
    )
    far_z = jnp.einsum(
        "sl,lyx->syx", far_rows, coarse, preferred_element_type=jnp.float32
    ).astype(jnp.bfloat16)
    for k in range(1, group):
        sent = far_z[(k - 1) * piece : k * piece]
        got = lax.ppermute(sent, "zq", [(j, (j + k) % group) for j in range(group)])
        fwd_z = fwd_z + got.astype(jnp.float32)
    resid_z = (slices_z.astype(jnp.float32) - fwd_z).astype(jnp.bfloat16)
    pieces = [resid_z]
    rows = [lax.dynamic_slice_in_dim(band_z, zq * piece, piece, 0)]
    for k in range(1, group):
        pieces.append(lax.ppermute(resid_z, "zq", [(j, (j + k) % group) for j in range(group)]))
        src = (zq - k + group) % group
        rows.append(lax.dynamic_slice_in_dim(band_z, src * piece, piece, 0))
    corr_z = jnp.einsum(
        "sl,syx->lyx",
        jnp.concatenate(rows, 0),
        jnp.concatenate(pieces, 0),
        preferred_element_type=jnp.float32,
    )

    return volume + step_size * (corr_x + corr_y + corr_z)


def solution(mesh):
    nslab, nrep = mesh.devices.shape
    slab = ("zb", "zq")
    rep = ("zl", "co")

    def run(volume, *rest):
        group = BLOCK // (volume.shape[0] // nslab)
        inner = Mesh(
            mesh.devices.reshape(nslab // group, group, 2, nrep // 2), ("zb", "zq", "zl", "co")
        )
        return jax.shard_map(
            shards,
            mesh=inner,
            in_specs=(
                P(slab, rep, None),
                P(slab, rep, None),
                P(slab, None, None),
                P(slab, rep, None),
                P(),
                P(),
                P(),
            ),
            out_specs=P(slab, rep, None),
            check_vma=False,
        )(volume, *rest)

    return run
```

```python
import jax
import jax.numpy as jnp
from jax import lax
from jax.sharding import Mesh, PartitionSpec as P

BLOCK = 128
SLICES = 16


step_size = 0.5


def block_mats(profiles, profile_index, block_shift):
    kinds = profiles.shape[0]
    span = profiles.shape[2]
    onehot = (profile_index[:, None] == jnp.arange(kinds, dtype=jnp.int32)[None, :]).astype(
        jnp.float32
    )
    picked = jnp.einsum("bk,ksl->bsl", onehot, profiles, precision=lax.Precision.HIGHEST)
    columns = jnp.arange(span, dtype=jnp.int32)
    target = (columns[None, :] + block_shift[:, None]) % span
    moving = (target[:, :, None] == columns[None, None, :]).astype(jnp.float32)
    shifted = jnp.einsum("bsj,bjl->bsl", picked, moving, precision=lax.Precision.HIGHEST)
    return shifted.astype(jnp.bfloat16)


def banded_matrix(along):
    count = along.shape[0]
    identity = jnp.eye(count, dtype=jnp.bfloat16)
    return (along[:, :, None, :] * identity[:, None, :, None]).reshape(
        count * SLICES, count * BLOCK
    )


def halve(values, axis, me):
    half = values.shape[0] // 2
    keep = lax.dynamic_slice_in_dim(values, me * half, half, 0)
    give = lax.dynamic_slice_in_dim(values, (1 - me) * half, half, 0)
    got = lax.ppermute(give.astype(jnp.bfloat16), axis, [(0, 1), (1, 0)])
    return keep + got.astype(jnp.float32)


def double(values, axis, me):
    other = lax.ppermute(values, axis, [(0, 1), (1, 0)])
    low = jnp.where(me == 0, values, other)
    high = jnp.where(me == 0, other, values)
    return jnp.concatenate([low, high], 0)


def shards(volume, slices_x, slices_y, slices_z, profiles, profile_index, block_shift):
    planes, rows_here, width = volume.shape
    count_x = width // BLOCK
    count_y = slices_y.shape[1] // SLICES
    mats = block_mats(profiles, profile_index, block_shift)
    along_x = mats[:count_x]
    along_y = mats[count_x : count_x + count_y]
    along_z = mats[count_x + count_y :]
    coarse = volume.astype(jnp.bfloat16)

    banded_x = banded_matrix(along_x)
    flat_coarse = coarse.reshape(planes * rows_here, width)
    fwd_x = lax.dot_general(
        flat_coarse, banded_x, (((1,), (1,)), ((), ())), preferred_element_type=jnp.float32
    )
    resid_x = (
        slices_x.reshape(planes * rows_here, count_x * SLICES).astype(jnp.float32) - fwd_x
    ).astype(jnp.bfloat16)
    corr_x = jnp.dot(resid_x, banded_x, preferred_element_type=jnp.float32).reshape(
        planes, rows_here, width
    )

    zb = lax.axis_index("zb")
    zq = lax.axis_index("zq")
    group = lax.axis_size("zq")
    mat_z = lax.dynamic_index_in_dim(along_z, zb, 0, keepdims=False)
    band_z = lax.dynamic_slice_in_dim(mat_z, zq * planes, planes, 1)
    piece = SLICES // group
    own_rows = lax.dynamic_slice_in_dim(band_z, zq * piece, piece, 0)
    own_z = jnp.einsum("sl,lyx->syx", own_rows, coarse, preferred_element_type=jnp.float32)

    zl = lax.axis_index("zl")
    co = lax.axis_index("co")
    rep = zl * 2 + co
    band_y = lax.dynamic_slice_in_dim(along_y[0], rep * rows_here, rows_here, 1)
    half = planes // 2
    keep_y = jnp.einsum(
        "sl,zlx->zsx",
        band_y,
        lax.dynamic_slice_in_dim(coarse, co * half, half, 0),
        preferred_element_type=jnp.float32,
    )
    give_y = jnp.einsum(
        "sl,zlx->zsx",
        band_y,
        lax.dynamic_slice_in_dim(coarse, (1 - co) * half, half, 0),
        preferred_element_type=jnp.float32,
    ).astype(jnp.bfloat16)
    got_y = lax.ppermute(give_y, "co", [(0, 1), (1, 0)])
    own_z, got_y = lax.optimization_barrier((own_z, got_y))
    fwd_y = halve(keep_y + got_y.astype(jnp.float32), "zl", zl)
    part_z = planes // 4
    obs_y = lax.dynamic_slice_in_dim(slices_y, (co * 2 + zl) * part_z, part_z, 0)
    resid_y = (obs_y.astype(jnp.float32) - fwd_y).astype(jnp.bfloat16)
    resid_y = double(resid_y, "zl", zl)
    resid_y = double(resid_y, "co", co)
    corr_y = jnp.einsum("sl,zsx->zlx", band_y, resid_y, preferred_element_type=jnp.float32)

    far_rows = jnp.concatenate(
        [lax.dynamic_slice_in_dim(band_z, ((zq + k) % group) * piece, piece, 0) for k in range(1, group)],
        0,
    )
    far_z = jnp.einsum(
        "sl,lyx->syx", far_rows, coarse, preferred_element_type=jnp.float32
    ).astype(jnp.bfloat16)
    fwd_z = own_z
    for k in range(1, group):
        sent = far_z[(k - 1) * piece : k * piece]
        got = lax.ppermute(sent, "zq", [(j, (j + k) % group) for j in range(group)])
        fwd_z = fwd_z + got.astype(jnp.float32)
    resid_z = (slices_z.astype(jnp.float32) - fwd_z).astype(jnp.bfloat16)
    pieces = [resid_z]
    rows = [lax.dynamic_slice_in_dim(band_z, zq * piece, piece, 0)]
    for k in range(1, group):
        pieces.append(lax.ppermute(resid_z, "zq", [(j, (j + k) % group) for j in range(group)]))
        src = (zq - k + group) % group
        rows.append(lax.dynamic_slice_in_dim(band_z, src * piece, piece, 0))
    corr_z = jnp.einsum(
        "sl,syx->lyx",
        jnp.concatenate(rows, 0),
        jnp.concatenate(pieces, 0),
        preferred_element_type=jnp.float32,
    )

    return volume + step_size * (corr_x + corr_y + corr_z)


def solution(mesh):
    nslab, nrep = mesh.devices.shape
    slab = ("zb", "zq")
    rep = ("zl", "co")

    def run(volume, *rest):
        group = BLOCK // (volume.shape[0] // nslab)
        inner = Mesh(
            mesh.devices.reshape(nslab // group, group, 2, nrep // 2), ("zb", "zq", "zl", "co")
        )
        return jax.shard_map(
            shards,
            mesh=inner,
            in_specs=(
                P(slab, rep, None),
                P(slab, rep, None),
                P(slab, None, None),
                P(slab, rep, None),
                P(),
                P(),
                P(),
            ),
            out_specs=P(slab, rep, None),
            check_vma=False,
        )(volume, *rest)

    return run
```

```python
import jax
import jax.numpy as jnp
from jax import lax
from jax.sharding import Mesh, PartitionSpec as P

BLOCK = 128
SLICES = 16


step_size = 0.5


def block_mats(profiles, profile_index, block_shift):
    kinds = profiles.shape[0]
    span = profiles.shape[2]
    onehot = (profile_index[:, None] == jnp.arange(kinds, dtype=jnp.int32)[None, :]).astype(
        jnp.float32
    )
    picked = jnp.einsum("bk,ksl->bsl", onehot, profiles, precision=lax.Precision.HIGHEST)
    columns = jnp.arange(span, dtype=jnp.int32)
    target = (columns[None, :] + block_shift[:, None]) % span
    moving = (target[:, :, None] == columns[None, None, :]).astype(jnp.float32)
    shifted = jnp.einsum("bsj,bjl->bsl", picked, moving, precision=lax.Precision.HIGHEST)
    return shifted.astype(jnp.bfloat16)


def banded_matrix(along):
    count = along.shape[0]
    identity = jnp.eye(count, dtype=jnp.bfloat16)
    return (along[:, :, None, :] * identity[:, None, :, None]).reshape(
        count * SLICES, count * BLOCK
    )


def halve(values, axis, me):
    half = values.shape[0] // 2
    keep = lax.dynamic_slice_in_dim(values, me * half, half, 0)
    give = lax.dynamic_slice_in_dim(values, (1 - me) * half, half, 0)
    got = lax.ppermute(give.astype(jnp.bfloat16), axis, [(0, 1), (1, 0)])
    return keep + got.astype(jnp.float32)


def double(values, axis, me):
    other = lax.ppermute(values, axis, [(0, 1), (1, 0)])
    low = jnp.where(me == 0, values, other)
    high = jnp.where(me == 0, other, values)
    return jnp.concatenate([low, high], 0)


def shards(volume, slices_x, slices_y, slices_z, profiles, profile_index, block_shift):
    planes, rows_here, width = volume.shape
    count_x = width // BLOCK
    count_y = slices_y.shape[1] // SLICES
    mats = block_mats(profiles, profile_index, block_shift)
    along_x = mats[:count_x]
    along_y = mats[count_x : count_x + count_y]
    along_z = mats[count_x + count_y :]
    coarse = volume.astype(jnp.bfloat16)

    banded_x = banded_matrix(along_x)
    flat_coarse = coarse.reshape(planes * rows_here, width)
    fwd_x = lax.dot_general(
        flat_coarse, banded_x, (((1,), (1,)), ((), ())), preferred_element_type=jnp.float32
    )
    resid_x = (
        slices_x.reshape(planes * rows_here, count_x * SLICES).astype(jnp.float32) - fwd_x
    ).astype(jnp.bfloat16)
    corr_x = jnp.dot(resid_x, banded_x, preferred_element_type=jnp.float32).reshape(
        planes, rows_here, width
    )

    zl = lax.axis_index("zl")
    co = lax.axis_index("co")
    rep = zl * 2 + co
    band_y = lax.dynamic_slice_in_dim(along_y[0], rep * rows_here, rows_here, 1)
    half = planes // 2
    keep_y = jnp.einsum(
        "sl,zlx->zsx",
        band_y,
        lax.dynamic_slice_in_dim(coarse, co * half, half, 0),
        preferred_element_type=jnp.float32,
    )
    give_y = jnp.einsum(
        "sl,zlx->zsx",
        band_y,
        lax.dynamic_slice_in_dim(coarse, (1 - co) * half, half, 0),
        preferred_element_type=jnp.float32,
    ).astype(jnp.bfloat16)
    fwd_y = keep_y + lax.ppermute(give_y, "co", [(0, 1), (1, 0)]).astype(jnp.float32)
    fwd_y = halve(fwd_y, "zl", zl)
    part_z = planes // 4
    obs_y = lax.dynamic_slice_in_dim(slices_y, (co * 2 + zl) * part_z, part_z, 0)
    resid_y = (obs_y.astype(jnp.float32) - fwd_y).astype(jnp.bfloat16)
    resid_y = double(resid_y, "zl", zl)
    resid_y = double(resid_y, "co", co)
    corr_y = jnp.einsum("sl,zsx->zlx", band_y, resid_y, preferred_element_type=jnp.float32)

    zb = lax.axis_index("zb")
    zq = lax.axis_index("zq")
    group = lax.axis_size("zq")
    mat_z = lax.dynamic_index_in_dim(along_z, zb, 0, keepdims=False)
    band_z = lax.dynamic_slice_in_dim(mat_z, zq * planes, planes, 1)
    piece = SLICES // group
    own_rows = lax.dynamic_slice_in_dim(band_z, zq * piece, piece, 0)
    fwd_z = jnp.einsum("sl,lyx->syx", own_rows, coarse, preferred_element_type=jnp.float32)
    far_rows = jnp.concatenate(
        [lax.dynamic_slice_in_dim(band_z, ((zq + k) % group) * piece, piece, 0) for k in range(1, group)],
        0,
    )
    far_z = jnp.einsum(
        "sl,lyx->syx", far_rows, coarse, preferred_element_type=jnp.float32
    ).astype(jnp.bfloat16)
    for k in range(1, group):
        sent = far_z[(k - 1) * piece : k * piece]
        got = lax.ppermute(sent, "zq", [(j, (j + k) % group) for j in range(group)])
        fwd_z = fwd_z + got.astype(jnp.float32)
    resid_z = (slices_z.astype(jnp.float32) - fwd_z).astype(jnp.bfloat16)
    pieces = [resid_z]
    rows = [lax.dynamic_slice_in_dim(band_z, zq * piece, piece, 0)]
    for k in range(1, group):
        pieces.append(lax.ppermute(resid_z, "zq", [(j, (j + k) % group) for j in range(group)]))
        src = (zq - k + group) % group
        rows.append(lax.dynamic_slice_in_dim(band_z, src * piece, piece, 0))
    base, pieces[1] = lax.optimization_barrier(
        (volume + step_size * (corr_x + corr_y), pieces[1])
    )
    corr_z = jnp.einsum(
        "sl,syx->lyx",
        jnp.concatenate(rows, 0),
        jnp.concatenate(pieces, 0),
        preferred_element_type=jnp.float32,
    )

    return base + step_size * corr_z


def solution(mesh):
    nslab, nrep = mesh.devices.shape
    slab = ("zb", "zq")
    rep = ("zl", "co")

    def run(volume, *rest):
        group = BLOCK // (volume.shape[0] // nslab)
        inner = Mesh(
            mesh.devices.reshape(nslab // group, group, 2, nrep // 2), ("zb", "zq", "zl", "co")
        )
        return jax.shard_map(
            shards,
            mesh=inner,
            in_specs=(
                P(slab, rep, None),
                P(slab, rep, None),
                P(slab, None, None),
                P(slab, rep, None),
                P(),
                P(),
                P(),
            ),
            out_specs=P(slab, rep, None),
            check_vma=False,
        )(volume, *rest)

    return run
```

```python
import jax
import jax.numpy as jnp
from jax import lax
from jax.sharding import Mesh, PartitionSpec as P

BLOCK = 128
SLICES = 16


step_size = 0.5


def block_mats(profiles, profile_index, block_shift):
    kinds = profiles.shape[0]
    span = profiles.shape[2]
    onehot = (profile_index[:, None] == jnp.arange(kinds, dtype=jnp.int32)[None, :]).astype(
        jnp.float32
    )
    picked = jnp.einsum("bk,ksl->bsl", onehot, profiles, precision=lax.Precision.HIGHEST)
    columns = jnp.arange(span, dtype=jnp.int32)
    target = (columns[None, :] + block_shift[:, None]) % span
    moving = (target[:, :, None] == columns[None, None, :]).astype(jnp.float32)
    shifted = jnp.einsum("bsj,bjl->bsl", picked, moving, precision=lax.Precision.HIGHEST)
    return shifted.astype(jnp.bfloat16)


def banded_matrix(along):
    count = along.shape[0]
    identity = jnp.eye(count, dtype=jnp.bfloat16)
    return (along[:, :, None, :] * identity[:, None, :, None]).reshape(
        count * SLICES, count * BLOCK
    )


def halve(values, axis, me):
    half = values.shape[0] // 2
    keep = lax.dynamic_slice_in_dim(values, me * half, half, 0)
    give = lax.dynamic_slice_in_dim(values, (1 - me) * half, half, 0)
    got = lax.ppermute(give.astype(jnp.bfloat16), axis, [(0, 1), (1, 0)])
    return keep + got.astype(jnp.float32)


def double(values, axis, me):
    other = lax.ppermute(values, axis, [(0, 1), (1, 0)])
    low = jnp.where(me == 0, values, other)
    high = jnp.where(me == 0, other, values)
    return jnp.concatenate([low, high], 0)


def shards(volume, slices_x, slices_y, slices_z, profiles, profile_index, block_shift):
    planes, rows_here, width = volume.shape
    count_x = width // BLOCK
    count_y = slices_y.shape[1] // SLICES
    mats = block_mats(profiles, profile_index, block_shift)
    along_x = mats[:count_x]
    along_y = mats[count_x : count_x + count_y]
    along_z = mats[count_x + count_y :]
    coarse = volume.astype(jnp.bfloat16)

    banded_x = banded_matrix(along_x)
    flat_coarse = coarse.reshape(planes * rows_here, width)
    fwd_x = lax.dot_general(
        flat_coarse, banded_x, (((1,), (1,)), ((), ())), preferred_element_type=jnp.float32
    )
    resid_x = (
        slices_x.reshape(planes * rows_here, count_x * SLICES).astype(jnp.float32) - fwd_x
    ).astype(jnp.bfloat16)
    corr_x = jnp.dot(resid_x, banded_x, preferred_element_type=jnp.float32).reshape(
        planes, rows_here, width
    )

    zl = lax.axis_index("zl")
    co = lax.axis_index("co")
    rep = zl * 2 + co
    band_y = lax.dynamic_slice_in_dim(along_y[0], rep * rows_here, rows_here, 1)
    nrep = 4
    part_z = planes // nrep
    axes = ("zl", "co")
    chunks = jnp.einsum(
        "sl,zlx->zsx", band_y, coarse, preferred_element_type=jnp.float32
    ).reshape(nrep, part_z, SLICES, width)
    fwd_y = lax.dynamic_index_in_dim(chunks, rep, 0, keepdims=False)
    for k in range(1, nrep):
        sent = lax.dynamic_index_in_dim(chunks, (rep + k) % nrep, 0, keepdims=False)
        got = lax.ppermute(sent.astype(jnp.bfloat16), axes, [(j, (j + k) % nrep) for j in range(nrep)])
        fwd_y = fwd_y + got.astype(jnp.float32)
    obs_y = lax.dynamic_slice_in_dim(slices_y, rep * part_z, part_z, 0)
    resid_y = (obs_y.astype(jnp.float32) - fwd_y).astype(jnp.bfloat16)
    placed = [resid_y]
    for k in range(1, nrep):
        placed.append(lax.ppermute(resid_y, axes, [(j, (j + k) % nrep) for j in range(nrep)]))
    order = [(nrep - ((t - rep) % nrep)) % nrep for t in range(nrep)]
    stacked = jnp.stack(placed, 0)
    resid_y = jnp.concatenate(
        [lax.dynamic_index_in_dim(stacked, order[t], 0, keepdims=False) for t in range(nrep)], 0
    )
    corr_y = jnp.einsum("sl,zsx->zlx", band_y, resid_y, preferred_element_type=jnp.float32)

    zb = lax.axis_index("zb")
    zq = lax.axis_index("zq")
    group = lax.axis_size("zq")
    mat_z = lax.dynamic_index_in_dim(along_z, zb, 0, keepdims=False)
    band_z = lax.dynamic_slice_in_dim(mat_z, zq * planes, planes, 1)
    piece = SLICES // group
    own_rows = lax.dynamic_slice_in_dim(band_z, zq * piece, piece, 0)
    fwd_z = jnp.einsum("sl,lyx->syx", own_rows, coarse, preferred_element_type=jnp.float32)
    far_rows = jnp.concatenate(
        [lax.dynamic_slice_in_dim(band_z, ((zq + k) % group) * piece, piece, 0) for k in range(1, group)],
        0,
    )
    far_z = jnp.einsum(
        "sl,lyx->syx", far_rows, coarse, preferred_element_type=jnp.float32
    ).astype(jnp.bfloat16)
    for k in range(1, group):
        sent = far_z[(k - 1) * piece : k * piece]
        got = lax.ppermute(sent, "zq", [(j, (j + k) % group) for j in range(group)])
        fwd_z = fwd_z + got.astype(jnp.float32)
    resid_z = (slices_z.astype(jnp.float32) - fwd_z).astype(jnp.bfloat16)
    pieces = [resid_z]
    rows = [lax.dynamic_slice_in_dim(band_z, zq * piece, piece, 0)]
    for k in range(1, group):
        pieces.append(lax.ppermute(resid_z, "zq", [(j, (j + k) % group) for j in range(group)]))
        src = (zq - k + group) % group
        rows.append(lax.dynamic_slice_in_dim(band_z, src * piece, piece, 0))
    corr_z = jnp.einsum(
        "sl,syx->lyx",
        jnp.concatenate(rows, 0),
        jnp.concatenate(pieces, 0),
        preferred_element_type=jnp.float32,
    )

    return volume + step_size * (corr_x + corr_y + corr_z)


def solution(mesh):
    nslab, nrep = mesh.devices.shape
    slab = ("zb", "zq")
    rep = ("zl", "co")

    def run(volume, *rest):
        group = BLOCK // (volume.shape[0] // nslab)
        inner = Mesh(
            mesh.devices.reshape(nslab // group, group, 2, nrep // 2), ("zb", "zq", "zl", "co")
        )
        return jax.shard_map(
            shards,
            mesh=inner,
            in_specs=(
                P(slab, rep, None),
                P(slab, rep, None),
                P(slab, None, None),
                P(slab, rep, None),
                P(),
                P(),
                P(),
            ),
            out_specs=P(slab, rep, None),
            check_vma=False,
        )(volume, *rest)

    return run
```

```python
import jax
import jax.numpy as jnp
from jax import lax
from jax.sharding import Mesh, PartitionSpec as P

BLOCK = 128
SLICES = 16


step_size = 0.5


def block_mats(profiles, profile_index, block_shift):
    kinds = profiles.shape[0]
    span = profiles.shape[2]
    onehot = (profile_index[:, None] == jnp.arange(kinds, dtype=jnp.int32)[None, :]).astype(
        jnp.float32
    )
    picked = jnp.einsum("bk,ksl->bsl", onehot, profiles, precision=lax.Precision.HIGHEST)
    columns = jnp.arange(span, dtype=jnp.int32)
    target = (columns[None, :] + block_shift[:, None]) % span
    moving = (target[:, :, None] == columns[None, None, :]).astype(jnp.float32)
    shifted = jnp.einsum("bsj,bjl->bsl", picked, moving, precision=lax.Precision.HIGHEST)
    return shifted.astype(jnp.bfloat16)


def banded_matrix(along):
    count = along.shape[0]
    identity = jnp.eye(count, dtype=jnp.bfloat16)
    return (along[:, :, None, :] * identity[:, None, :, None]).reshape(
        count * SLICES, count * BLOCK
    )


def halve(values, axis, me):
    half = values.shape[0] // 2
    keep = lax.dynamic_slice_in_dim(values, me * half, half, 0)
    give = lax.dynamic_slice_in_dim(values, (1 - me) * half, half, 0)
    got = lax.ppermute(give.astype(jnp.bfloat16), axis, [(0, 1), (1, 0)])
    return keep + got.astype(jnp.float32)


def double(values, axis, me):
    other = lax.ppermute(values, axis, [(0, 1), (1, 0)])
    low = jnp.where(me == 0, values, other)
    high = jnp.where(me == 0, other, values)
    return jnp.concatenate([low, high], 0)


def shards(volume, slices_x, slices_y, slices_z, profiles, profile_index, block_shift):
    planes, rows_here, width = volume.shape
    count_x = width // BLOCK
    count_y = slices_y.shape[1] // SLICES
    mats = block_mats(profiles, profile_index, block_shift)
    along_x = mats[:count_x]
    along_y = mats[count_x : count_x + count_y]
    along_z = mats[count_x + count_y :]
    coarse = volume.astype(jnp.bfloat16)

    banded_x = banded_matrix(along_x)
    flat_coarse = coarse.reshape(planes * rows_here, width)
    fwd_x = lax.dot_general(
        flat_coarse, banded_x, (((1,), (1,)), ((), ())), preferred_element_type=jnp.float32
    )
    resid_x = (
        slices_x.reshape(planes * rows_here, count_x * SLICES).astype(jnp.float32) - fwd_x
    ).astype(jnp.bfloat16)
    corr_x = jnp.dot(resid_x, banded_x, preferred_element_type=jnp.float32).reshape(
        planes, rows_here, width
    )

    zl = lax.axis_index("zl")
    co = lax.axis_index("co")
    rep = zl * 2 + co
    band_y = lax.dynamic_slice_in_dim(along_y[0], rep * rows_here, rows_here, 1)
    half = planes // 2
    keep_y = jnp.einsum(
        "sl,zlx->zsx",
        band_y,
        lax.dynamic_slice_in_dim(coarse, co * half, half, 0),
        preferred_element_type=jnp.float32,
    )
    give_y = jnp.einsum(
        "sl,zlx->zsx",
        band_y,
        lax.dynamic_slice_in_dim(coarse, (1 - co) * half, half, 0),
        preferred_element_type=jnp.float32,
    ).astype(jnp.bfloat16)
    fwd_y = keep_y + lax.ppermute(give_y, "co", [(0, 1), (1, 0)]).astype(jnp.float32)
    fwd_y = halve(fwd_y, "zl", zl)
    part_z = planes // 4
    obs_y = lax.dynamic_slice_in_dim(slices_y, (co * 2 + zl) * part_z, part_z, 0)
    resid_y = (obs_y.astype(jnp.float32) - fwd_y).astype(jnp.bfloat16)
    resid_y = double(resid_y, "zl", zl)
    resid_y = double(resid_y, "co", co)
    corr_y = jnp.einsum("sl,zsx->zlx", band_y, resid_y, preferred_element_type=jnp.float32)

    zb = lax.axis_index("zb")
    zq = lax.axis_index("zq")
    group = lax.axis_size("zq")
    mat_z = lax.dynamic_index_in_dim(along_z, zb, 0, keepdims=False)
    band_z = lax.dynamic_slice_in_dim(mat_z, zq * planes, planes, 1)
    piece = SLICES // group
    full_z = jnp.einsum(
        "sl,lyx->syx", band_z, coarse, preferred_element_type=jnp.float32
    ).reshape((group, piece) + coarse.shape[1:])
    came = lax.all_to_all(full_z.astype(jnp.bfloat16), "zq", 0, 0, tiled=True)
    others = (jnp.arange(group) != zq)[:, None, None, None]
    fwd_z = jnp.sum(jnp.where(others, came.astype(jnp.float32), 0.0), 0)
    fwd_z = fwd_z + lax.dynamic_index_in_dim(full_z, zq, 0, keepdims=False)
    resid_z = (slices_z.astype(jnp.float32) - fwd_z).astype(jnp.bfloat16)
    every = jnp.broadcast_to(resid_z[None], (group,) + resid_z.shape)
    gathered = lax.all_to_all(every, "zq", 0, 0, tiled=True).reshape(
        (SLICES,) + resid_z.shape[1:]
    )
    corr_z = jnp.einsum("sl,syx->lyx", band_z, gathered, preferred_element_type=jnp.float32)

    return volume + step_size * (corr_x + corr_y + corr_z)


def solution(mesh):
    nslab, nrep = mesh.devices.shape
    slab = ("zb", "zq")
    rep = ("zl", "co")

    def run(volume, *rest):
        group = BLOCK // (volume.shape[0] // nslab)
        inner = Mesh(
            mesh.devices.reshape(nslab // group, group, 2, nrep // 2), ("zb", "zq", "zl", "co")
        )
        return jax.shard_map(
            shards,
            mesh=inner,
            in_specs=(
                P(slab, rep, None),
                P(slab, rep, None),
                P(slab, None, None),
                P(slab, rep, None),
                P(),
                P(),
                P(),
            ),
            out_specs=P(slab, rep, None),
            check_vma=False,
        )(volume, *rest)

    return run
```

```python
import jax
import jax.numpy as jnp
from jax import lax
from jax.sharding import Mesh, PartitionSpec as P

BLOCK = 128
SLICES = 16


step_size = 0.5


def block_mats(profiles, profile_index, block_shift):
    kinds = profiles.shape[0]
    span = profiles.shape[2]
    onehot = (profile_index[:, None] == jnp.arange(kinds, dtype=jnp.int32)[None, :]).astype(
        jnp.float32
    )
    picked = jnp.einsum("bk,ksl->bsl", onehot, profiles, precision=lax.Precision.HIGHEST)
    columns = jnp.arange(span, dtype=jnp.int32)
    target = (columns[None, :] + block_shift[:, None]) % span
    moving = (target[:, :, None] == columns[None, None, :]).astype(jnp.float32)
    shifted = jnp.einsum("bsj,bjl->bsl", picked, moving, precision=lax.Precision.HIGHEST)
    return shifted.astype(jnp.bfloat16)


def banded_matrix(along):
    count = along.shape[0]
    identity = jnp.eye(count, dtype=jnp.bfloat16)
    return (along[:, :, None, :] * identity[:, None, :, None]).reshape(
        count * SLICES, count * BLOCK
    )


def halve(values, axis, me):
    half = values.shape[0] // 2
    keep = lax.dynamic_slice_in_dim(values, me * half, half, 0)
    give = lax.dynamic_slice_in_dim(values, (1 - me) * half, half, 0)
    got = lax.ppermute(give.astype(jnp.bfloat16), axis, [(0, 1), (1, 0)])
    return keep + got.astype(jnp.float32)


def double(values, axis, me):
    other = lax.ppermute(values, axis, [(0, 1), (1, 0)])
    low = jnp.where(me == 0, values, other)
    high = jnp.where(me == 0, other, values)
    return jnp.concatenate([low, high], 0)


def shards(volume, slices_x, slices_y, slices_z, profiles, profile_index, block_shift):
    planes, rows_here, width = volume.shape
    count_x = width // BLOCK
    count_y = slices_y.shape[1] // SLICES
    mats = block_mats(profiles, profile_index, block_shift)
    along_x = mats[:count_x]
    along_y = mats[count_x : count_x + count_y]
    along_z = mats[count_x + count_y :]
    coarse = volume.astype(jnp.bfloat16)

    banded_x = banded_matrix(along_x)
    flat_coarse = coarse.reshape(planes * rows_here, width)
    fwd_x = lax.dot_general(
        flat_coarse, banded_x, (((1,), (1,)), ((), ())), preferred_element_type=jnp.float32
    )
    resid_x = (
        slices_x.reshape(planes * rows_here, count_x * SLICES).astype(jnp.float32) - fwd_x
    ).astype(jnp.bfloat16)
    corr_x = jnp.dot(resid_x, banded_x, preferred_element_type=jnp.float32).reshape(
        planes, rows_here, width
    )

    zl = lax.axis_index("zl")
    co = lax.axis_index("co")
    rep = zl * 2 + co
    band_y = lax.dynamic_slice_in_dim(along_y[0], rep * rows_here, rows_here, 1)
    half = planes // 2
    keep_y = jnp.einsum(
        "sl,zlx->zsx",
        band_y,
        lax.dynamic_slice_in_dim(coarse, co * half, half, 0),
        preferred_element_type=jnp.float32,
    )
    give_y = jnp.einsum(
        "sl,zlx->zsx",
        band_y,
        lax.dynamic_slice_in_dim(coarse, (1 - co) * half, half, 0),
        preferred_element_type=jnp.float32,
    ).astype(jnp.bfloat16)
    fwd_y = keep_y + lax.ppermute(give_y, "co", [(0, 1), (1, 0)]).astype(jnp.float32)
    fwd_y = halve(fwd_y, "zl", zl)
    part_z = planes // 4
    obs_y = lax.dynamic_slice_in_dim(slices_y, (co * 2 + zl) * part_z, part_z, 0)
    resid_y = (obs_y.astype(jnp.float32) - fwd_y).astype(jnp.bfloat16)
    resid_y = double(resid_y, "zl", zl)
    resid_y = double(resid_y, "co", co)
    corr_y = jnp.einsum("sl,zsx->zlx", band_y, resid_y, preferred_element_type=jnp.float32)

    zb = lax.axis_index("zb")
    zq = lax.axis_index("zq")
    group = lax.axis_size("zq")
    mat_z = lax.dynamic_index_in_dim(along_z, zb, 0, keepdims=False)
    band_z = lax.dynamic_slice_in_dim(mat_z, zq * planes, planes, 1)
    piece = SLICES // group
    sheet = coarse.reshape(planes, rows_here * width)
    own_rows = lax.dynamic_slice_in_dim(band_z, zq * piece, piece, 0)
    fwd_z = jnp.dot(own_rows, sheet, preferred_element_type=jnp.float32)
    far_rows = jnp.concatenate(
        [lax.dynamic_slice_in_dim(band_z, ((zq + k) % group) * piece, piece, 0) for k in range(1, group)],
        0,
    )
    far_z = jnp.dot(far_rows, sheet, preferred_element_type=jnp.float32).astype(jnp.bfloat16)
    for k in range(1, group):
        sent = far_z[(k - 1) * piece : k * piece]
        got = lax.ppermute(sent, "zq", [(j, (j + k) % group) for j in range(group)])
        fwd_z = fwd_z + got.astype(jnp.float32)
    observed = slices_z.reshape(piece, rows_here * width).astype(jnp.float32)
    resid_z = (observed - fwd_z).astype(jnp.bfloat16)
    pieces = [resid_z]
    rows = [own_rows]
    for k in range(1, group):
        pieces.append(lax.ppermute(resid_z, "zq", [(j, (j + k) % group) for j in range(group)]))
        src = (zq - k + group) % group
        rows.append(lax.dynamic_slice_in_dim(band_z, src * piece, piece, 0))
    corr_z = lax.dot_general(
        jnp.concatenate(rows, 0),
        jnp.concatenate(pieces, 0),
        (((0,), (0,)), ((), ())),
        preferred_element_type=jnp.float32,
    ).reshape(planes, rows_here, width)

    return volume + step_size * (corr_x + corr_y + corr_z)


def solution(mesh):
    nslab, nrep = mesh.devices.shape
    slab = ("zb", "zq")
    rep = ("zl", "co")

    def run(volume, *rest):
        group = BLOCK // (volume.shape[0] // nslab)
        inner = Mesh(
            mesh.devices.reshape(nslab // group, group, 2, nrep // 2), ("zb", "zq", "zl", "co")
        )
        return jax.shard_map(
            shards,
            mesh=inner,
            in_specs=(
                P(slab, rep, None),
                P(slab, rep, None),
                P(slab, None, None),
                P(slab, rep, None),
                P(),
                P(),
                P(),
            ),
            out_specs=P(slab, rep, None),
            check_vma=False,
        )(volume, *rest)

    return run
```

```python
import jax
import jax.numpy as jnp
from jax import lax
from jax.sharding import Mesh, PartitionSpec as P

BLOCK = 128
SLICES = 16


step_size = 0.5


def block_mats(profiles, profile_index, block_shift):
    kinds = profiles.shape[0]
    span = profiles.shape[2]
    onehot = (profile_index[:, None] == jnp.arange(kinds, dtype=jnp.int32)[None, :]).astype(
        jnp.float32
    )
    picked = jnp.einsum("bk,ksl->bsl", onehot, profiles, precision=lax.Precision.HIGHEST)
    columns = jnp.arange(span, dtype=jnp.int32)
    target = (columns[None, :] + block_shift[:, None]) % span
    moving = (target[:, :, None] == columns[None, None, :]).astype(jnp.float32)
    shifted = jnp.einsum("bsj,bjl->bsl", picked, moving, precision=lax.Precision.HIGHEST)
    return shifted.astype(jnp.bfloat16)


def one_band(profiles, profile_index, block_shift, block):
    span = profiles.shape[2]
    picked = lax.dynamic_index_in_dim(profiles, profile_index[block], 0, keepdims=False)
    doubled = jnp.concatenate([picked, picked], 1)
    shift = block_shift[block] % span
    return lax.dynamic_slice_in_dim(doubled, span - shift, span, 1).astype(jnp.bfloat16)


def banded_matrix(along):
    count = along.shape[0]
    identity = jnp.eye(count, dtype=jnp.bfloat16)
    return (along[:, :, None, :] * identity[:, None, :, None]).reshape(
        count * SLICES, count * BLOCK
    )


def halve(values, axis, me):
    half = values.shape[0] // 2
    keep = lax.dynamic_slice_in_dim(values, me * half, half, 0)
    give = lax.dynamic_slice_in_dim(values, (1 - me) * half, half, 0)
    got = lax.ppermute(give.astype(jnp.bfloat16), axis, [(0, 1), (1, 0)])
    return keep + got.astype(jnp.float32)


def double(values, axis, me):
    other = lax.ppermute(values, axis, [(0, 1), (1, 0)])
    low = jnp.where(me == 0, values, other)
    high = jnp.where(me == 0, other, values)
    return jnp.concatenate([low, high], 0)


def shards(volume, slices_x, slices_y, slices_z, profiles, profile_index, block_shift):
    planes, rows_here, width = volume.shape
    count_x = width // BLOCK
    count_y = slices_y.shape[1] // SLICES
    mats = block_mats(profiles, profile_index, block_shift)
    along_x = mats[:count_x]
    coarse = volume.astype(jnp.bfloat16)

    banded_x = banded_matrix(along_x)
    flat_coarse = coarse.reshape(planes * rows_here, width)
    fwd_x = lax.dot_general(
        flat_coarse, banded_x, (((1,), (1,)), ((), ())), preferred_element_type=jnp.float32
    )
    resid_x = (
        slices_x.reshape(planes * rows_here, count_x * SLICES).astype(jnp.float32) - fwd_x
    ).astype(jnp.bfloat16)
    corr_x = jnp.dot(resid_x, banded_x, preferred_element_type=jnp.float32).reshape(
        planes, rows_here, width
    )

    zl = lax.axis_index("zl")
    co = lax.axis_index("co")
    rep = zl * 2 + co
    mat_y = one_band(profiles, profile_index, block_shift, count_x)
    band_y = lax.dynamic_slice_in_dim(mat_y, rep * rows_here, rows_here, 1)
    half = planes // 2
    keep_y = jnp.einsum(
        "sl,zlx->zsx",
        band_y,
        lax.dynamic_slice_in_dim(coarse, co * half, half, 0),
        preferred_element_type=jnp.float32,
    )
    give_y = jnp.einsum(
        "sl,zlx->zsx",
        band_y,
        lax.dynamic_slice_in_dim(coarse, (1 - co) * half, half, 0),
        preferred_element_type=jnp.float32,
    ).astype(jnp.bfloat16)
    fwd_y = keep_y + lax.ppermute(give_y, "co", [(0, 1), (1, 0)]).astype(jnp.float32)
    fwd_y = halve(fwd_y, "zl", zl)
    part_z = planes // 4
    obs_y = lax.dynamic_slice_in_dim(slices_y, (co * 2 + zl) * part_z, part_z, 0)
    resid_y = (obs_y.astype(jnp.float32) - fwd_y).astype(jnp.bfloat16)
    resid_y = double(resid_y, "zl", zl)
    resid_y = double(resid_y, "co", co)
    corr_y = jnp.einsum("sl,zsx->zlx", band_y, resid_y, preferred_element_type=jnp.float32)

    zb = lax.axis_index("zb")
    zq = lax.axis_index("zq")
    group = lax.axis_size("zq")
    mat_z = one_band(profiles, profile_index, block_shift, count_x + count_y + zb)
    band_z = lax.dynamic_slice_in_dim(mat_z, zq * planes, planes, 1)
    piece = SLICES // group
    sheet = coarse.reshape(planes, rows_here * width)
    own_rows = lax.dynamic_slice_in_dim(band_z, zq * piece, piece, 0)
    fwd_z = jnp.dot(own_rows, sheet, preferred_element_type=jnp.float32)
    far_rows = jnp.concatenate(
        [lax.dynamic_slice_in_dim(band_z, ((zq + k) % group) * piece, piece, 0) for k in range(1, group)],
        0,
    )
    far_z = jnp.dot(far_rows, sheet, preferred_element_type=jnp.float32).astype(jnp.bfloat16)
    for k in range(1, group):
        sent = far_z[(k - 1) * piece : k * piece]
        got = lax.ppermute(sent, "zq", [(j, (j + k) % group) for j in range(group)])
        fwd_z = fwd_z + got.astype(jnp.float32)
    observed = slices_z.reshape(piece, rows_here * width).astype(jnp.float32)
    resid_z = (observed - fwd_z).astype(jnp.bfloat16)
    pieces = [resid_z]
    rows = [own_rows]
    for k in range(1, group):
        pieces.append(lax.ppermute(resid_z, "zq", [(j, (j + k) % group) for j in range(group)]))
        src = (zq - k + group) % group
        rows.append(lax.dynamic_slice_in_dim(band_z, src * piece, piece, 0))
    corr_z = lax.dot_general(
        jnp.concatenate(rows, 0),
        jnp.concatenate(pieces, 0),
        (((0,), (0,)), ((), ())),
        preferred_element_type=jnp.float32,
    ).reshape(planes, rows_here, width)

    return volume + step_size * (corr_x + corr_y + corr_z)


def solution(mesh):
    nslab, nrep = mesh.devices.shape
    slab = ("zb", "zq")
    rep = ("zl", "co")

    def run(volume, *rest):
        group = BLOCK // (volume.shape[0] // nslab)
        inner = Mesh(
            mesh.devices.reshape(nslab // group, group, 2, nrep // 2), ("zb", "zq", "zl", "co")
        )
        return jax.shard_map(
            shards,
            mesh=inner,
            in_specs=(
                P(slab, rep, None),
                P(slab, rep, None),
                P(slab, None, None),
                P(slab, rep, None),
                P(),
                P(),
                P(),
            ),
            out_specs=P(slab, rep, None),
            check_vma=False,
        )(volume, *rest)

    return run
```

```python
import jax
import jax.numpy as jnp
from jax import lax
from jax.sharding import Mesh, PartitionSpec as P

BLOCK = 128
SLICES = 16


step_size = 0.5


def block_mats(profiles, profile_index, block_shift):
    kinds = profiles.shape[0]
    span = profiles.shape[2]
    onehot = (profile_index[:, None] == jnp.arange(kinds, dtype=jnp.int32)[None, :]).astype(
        jnp.float32
    )
    picked = jnp.einsum("bk,ksl->bsl", onehot, profiles, precision=lax.Precision.HIGHEST)
    columns = jnp.arange(span, dtype=jnp.int32)
    target = (columns[None, :] + block_shift[:, None]) % span
    moving = (target[:, :, None] == columns[None, None, :]).astype(jnp.float32)
    shifted = jnp.einsum("bsj,bjl->bsl", picked, moving, precision=lax.Precision.HIGHEST)
    return shifted.astype(jnp.bfloat16)


def spread(band, rows):
    eye = jnp.eye(rows, dtype=band.dtype)
    outer, inner = band.shape
    return (band[:, None, :, None] * eye[None, :, None, :]).reshape(outer * rows, inner * rows)


def banded_matrix(along):
    count = along.shape[0]
    identity = jnp.eye(count, dtype=jnp.bfloat16)
    return (along[:, :, None, :] * identity[:, None, :, None]).reshape(
        count * SLICES, count * BLOCK
    )


def halve(values, axis, me):
    half = values.shape[0] // 2
    keep = lax.dynamic_slice_in_dim(values, me * half, half, 0)
    give = lax.dynamic_slice_in_dim(values, (1 - me) * half, half, 0)
    got = lax.ppermute(give.astype(jnp.bfloat16), axis, [(0, 1), (1, 0)])
    return keep + got.astype(jnp.float32)


def double(values, axis, me):
    other = lax.ppermute(values, axis, [(0, 1), (1, 0)])
    low = jnp.where(me == 0, values, other)
    high = jnp.where(me == 0, other, values)
    return jnp.concatenate([low, high], 0)


def shards(volume, slices_x, slices_y, slices_z, profiles, profile_index, block_shift):
    planes, rows_here, width = volume.shape
    count_x = width // BLOCK
    count_y = slices_y.shape[1] // SLICES
    mats = block_mats(profiles, profile_index, block_shift)
    along_x = mats[:count_x]
    along_y = mats[count_x : count_x + count_y]
    along_z = mats[count_x + count_y :]
    coarse = volume.astype(jnp.bfloat16)

    banded_x = banded_matrix(along_x)
    flat_coarse = coarse.reshape(planes * rows_here, width)
    fwd_x = lax.dot_general(
        flat_coarse, banded_x, (((1,), (1,)), ((), ())), preferred_element_type=jnp.float32
    )
    resid_x = (
        slices_x.reshape(planes * rows_here, count_x * SLICES).astype(jnp.float32) - fwd_x
    ).astype(jnp.bfloat16)
    corr_x = jnp.dot(resid_x, banded_x, preferred_element_type=jnp.float32).reshape(
        planes, rows_here, width
    )

    zl = lax.axis_index("zl")
    co = lax.axis_index("co")
    rep = zl * 2 + co
    band_y = lax.dynamic_slice_in_dim(along_y[0], rep * rows_here, rows_here, 1)
    half = planes // 2
    keep_y = jnp.einsum(
        "sl,zlx->zsx",
        band_y,
        lax.dynamic_slice_in_dim(coarse, co * half, half, 0),
        preferred_element_type=jnp.float32,
    )
    give_y = jnp.einsum(
        "sl,zlx->zsx",
        band_y,
        lax.dynamic_slice_in_dim(coarse, (1 - co) * half, half, 0),
        preferred_element_type=jnp.float32,
    ).astype(jnp.bfloat16)
    fwd_y = keep_y + lax.ppermute(give_y, "co", [(0, 1), (1, 0)]).astype(jnp.float32)
    fwd_y = halve(fwd_y, "zl", zl)
    part_z = planes // 4
    obs_y = lax.dynamic_slice_in_dim(slices_y, (co * 2 + zl) * part_z, part_z, 0)
    resid_y = (obs_y.astype(jnp.float32) - fwd_y).astype(jnp.bfloat16)
    resid_y = double(resid_y, "zl", zl)
    resid_y = double(resid_y, "co", co)
    corr_y = jnp.einsum("sl,zsx->zlx", band_y, resid_y, preferred_element_type=jnp.float32)

    zb = lax.axis_index("zb")
    zq = lax.axis_index("zq")
    group = lax.axis_size("zq")
    mat_z = lax.dynamic_index_in_dim(along_z, zb, 0, keepdims=False)
    band_z = lax.dynamic_slice_in_dim(mat_z, zq * planes, planes, 1)
    piece = SLICES // group
    sheet = coarse.reshape(planes * rows_here, width)
    own_rows = lax.dynamic_slice_in_dim(band_z, zq * piece, piece, 0)
    fwd_z = jnp.dot(spread(own_rows, rows_here), sheet, preferred_element_type=jnp.float32)
    far_rows = jnp.concatenate(
        [lax.dynamic_slice_in_dim(band_z, ((zq + k) % group) * piece, piece, 0) for k in range(1, group)],
        0,
    )
    far_z = jnp.dot(
        spread(far_rows, rows_here), sheet, preferred_element_type=jnp.float32
    ).astype(jnp.bfloat16)
    block = piece * rows_here
    for k in range(1, group):
        sent = far_z[(k - 1) * block : k * block]
        got = lax.ppermute(sent, "zq", [(j, (j + k) % group) for j in range(group)])
        fwd_z = fwd_z + got.astype(jnp.float32)
    observed = slices_z.reshape(block, width).astype(jnp.float32)
    resid_z = (observed - fwd_z).astype(jnp.bfloat16)
    pieces = [resid_z]
    rows = [own_rows]
    for k in range(1, group):
        pieces.append(lax.ppermute(resid_z, "zq", [(j, (j + k) % group) for j in range(group)]))
        src = (zq - k + group) % group
        rows.append(lax.dynamic_slice_in_dim(band_z, src * piece, piece, 0))
    corr_z = jnp.dot(
        spread(jnp.concatenate(rows, 0).T, rows_here),
        jnp.concatenate(pieces, 0),
        preferred_element_type=jnp.float32,
    ).reshape(planes, rows_here, width)

    return volume + step_size * (corr_x + corr_y + corr_z)


def solution(mesh):
    nslab, nrep = mesh.devices.shape
    slab = ("zb", "zq")
    rep = ("zl", "co")

    def run(volume, *rest):
        group = BLOCK // (volume.shape[0] // nslab)
        inner = Mesh(
            mesh.devices.reshape(nslab // group, group, 2, nrep // 2), ("zb", "zq", "zl", "co")
        )
        return jax.shard_map(
            shards,
            mesh=inner,
            in_specs=(
                P(slab, rep, None),
                P(slab, rep, None),
                P(slab, None, None),
                P(slab, rep, None),
                P(),
                P(),
                P(),
            ),
            out_specs=P(slab, rep, None),
            check_vma=False,
        )(volume, *rest)

    return run
```

```python
import jax
import jax.numpy as jnp
from jax import lax
from jax.sharding import Mesh, PartitionSpec as P

BLOCK = 128
SLICES = 16


step_size = 0.5


def block_mats(profiles, profile_index, block_shift):
    kinds = profiles.shape[0]
    span = profiles.shape[2]
    onehot = (profile_index[:, None] == jnp.arange(kinds, dtype=jnp.int32)[None, :]).astype(
        jnp.float32
    )
    picked = jnp.einsum("bk,ksl->bsl", onehot, profiles, precision=lax.Precision.HIGHEST)
    columns = jnp.arange(span, dtype=jnp.int32)
    target = (columns[None, :] + block_shift[:, None]) % span
    moving = (target[:, :, None] == columns[None, None, :]).astype(jnp.float32)
    shifted = jnp.einsum("bsj,bjl->bsl", picked, moving, precision=lax.Precision.HIGHEST)
    return shifted.astype(jnp.bfloat16)


def spread(band, rows):
    eye = jnp.eye(rows, dtype=band.dtype)
    outer, inner = band.shape
    return (band[:, None, :, None] * eye[None, :, None, :]).reshape(outer * rows, inner * rows)


def banded_matrix(along):
    count = along.shape[0]
    identity = jnp.eye(count, dtype=jnp.bfloat16)
    return (along[:, :, None, :] * identity[:, None, :, None]).reshape(
        count * SLICES, count * BLOCK
    )


def halve(values, axis, me):
    half = values.shape[0] // 2
    keep = lax.dynamic_slice_in_dim(values, me * half, half, 0)
    give = lax.dynamic_slice_in_dim(values, (1 - me) * half, half, 0)
    got = lax.ppermute(give.astype(jnp.bfloat16), axis, [(0, 1), (1, 0)])
    return keep + got.astype(jnp.float32)


def double(values, axis, me):
    other = lax.ppermute(values, axis, [(0, 1), (1, 0)])
    low = jnp.where(me == 0, values, other)
    high = jnp.where(me == 0, other, values)
    return jnp.concatenate([low, high], 0)


def shards(volume, slices_x, slices_y, slices_z, profiles, profile_index, block_shift):
    planes, rows_here, width = volume.shape
    count_x = width // BLOCK
    count_y = slices_y.shape[1] // SLICES
    mats = block_mats(profiles, profile_index, block_shift)
    along_x = mats[:count_x]
    along_y = mats[count_x : count_x + count_y]
    along_z = mats[count_x + count_y :]
    coarse = volume.astype(jnp.bfloat16)

    banded_x = banded_matrix(along_x)
    flat_coarse = coarse.reshape(planes * rows_here, width)
    fwd_x = lax.dot_general(
        flat_coarse, banded_x, (((1,), (1,)), ((), ())), preferred_element_type=jnp.float32
    )
    resid_x = (
        slices_x.reshape(planes * rows_here, count_x * SLICES).astype(jnp.float32) - fwd_x
    ).astype(jnp.bfloat16)
    corr_x = jnp.dot(resid_x, banded_x, preferred_element_type=jnp.float32).reshape(
        planes, rows_here, width
    )

    zl = lax.axis_index("zl")
    co = lax.axis_index("co")
    rep = zl * 2 + co
    band_y = lax.dynamic_slice_in_dim(along_y[0], rep * rows_here, rows_here, 1)
    half = planes // 2
    keep_y = jnp.einsum(
        "sl,zlx->zsx",
        band_y,
        lax.dynamic_slice_in_dim(coarse, co * half, half, 0),
        preferred_element_type=jnp.float32,
    )
    give_y = jnp.einsum(
        "sl,zlx->zsx",
        band_y,
        lax.dynamic_slice_in_dim(coarse, (1 - co) * half, half, 0),
        preferred_element_type=jnp.float32,
    ).astype(jnp.bfloat16)
    fwd_y = keep_y + lax.ppermute(give_y, "co", [(0, 1), (1, 0)]).astype(jnp.float32)
    fwd_y = halve(fwd_y, "zl", zl)
    part_z = planes // 4
    obs_y = lax.dynamic_slice_in_dim(slices_y, (co * 2 + zl) * part_z, part_z, 0)
    resid_y = (obs_y.astype(jnp.float32) - fwd_y).astype(jnp.bfloat16)
    resid_y = double(resid_y, "zl", zl)
    resid_y = double(resid_y, "co", co)
    corr_y = jnp.einsum("sl,zsx->zlx", band_y, resid_y, preferred_element_type=jnp.float32)

    zb = lax.axis_index("zb")
    zq = lax.axis_index("zq")
    group = lax.axis_size("zq")
    mat_z = lax.dynamic_index_in_dim(along_z, zb, 0, keepdims=False)
    band_z = lax.dynamic_slice_in_dim(mat_z, zq * planes, planes, 1)
    piece = SLICES // group
    sheet = coarse.reshape(planes, rows_here * width)
    own_rows = lax.dynamic_slice_in_dim(band_z, zq * piece, piece, 0)
    fwd_z = jnp.dot(own_rows, sheet, preferred_element_type=jnp.float32)
    far_rows = jnp.concatenate(
        [lax.dynamic_slice_in_dim(band_z, ((zq + k) % group) * piece, piece, 0) for k in range(1, group)],
        0,
    )
    far_z = jnp.dot(far_rows, sheet, preferred_element_type=jnp.float32).astype(jnp.bfloat16)
    for k in range(1, group):
        sent = far_z[(k - 1) * piece : k * piece]
        got = lax.ppermute(sent, "zq", [(j, (j + k) % group) for j in range(group)])
        fwd_z = fwd_z + got.astype(jnp.float32)
    fwd_z = fwd_z.reshape(slices_z.shape)
    resid_z = (slices_z.astype(jnp.float32) - fwd_z).astype(jnp.bfloat16)
    pieces = [resid_z]
    rows = [own_rows]
    for k in range(1, group):
        pieces.append(lax.ppermute(resid_z, "zq", [(j, (j + k) % group) for j in range(group)]))
        src = (zq - k + group) % group
        rows.append(lax.dynamic_slice_in_dim(band_z, src * piece, piece, 0))
    corr_z = jnp.dot(
        spread(jnp.concatenate(rows, 0).T, rows_here),
        jnp.concatenate(pieces, 0).reshape(SLICES * rows_here, width),
        preferred_element_type=jnp.float32,
    ).reshape(planes, rows_here, width)

    return volume + step_size * (corr_x + corr_y + corr_z)


def solution(mesh):
    nslab, nrep = mesh.devices.shape
    slab = ("zb", "zq")
    rep = ("zl", "co")

    def run(volume, *rest):
        group = BLOCK // (volume.shape[0] // nslab)
        inner = Mesh(
            mesh.devices.reshape(nslab // group, group, 2, nrep // 2), ("zb", "zq", "zl", "co")
        )
        return jax.shard_map(
            shards,
            mesh=inner,
            in_specs=(
                P(slab, rep, None),
                P(slab, rep, None),
                P(slab, None, None),
                P(slab, rep, None),
                P(),
                P(),
                P(),
            ),
            out_specs=P(slab, rep, None),
            check_vma=False,
        )(volume, *rest)

    return run
```

```python
import jax
import jax.numpy as jnp
from jax import lax
from jax.sharding import Mesh, PartitionSpec as P

BLOCK = 128
SLICES = 16


step_size = 0.5


def block_mats(profiles, profile_index, block_shift):
    kinds = profiles.shape[0]
    span = profiles.shape[2]
    onehot = (profile_index[:, None] == jnp.arange(kinds, dtype=jnp.int32)[None, :]).astype(
        jnp.float32
    )
    picked = jnp.einsum("bk,ksl->bsl", onehot, profiles, precision=lax.Precision.HIGHEST)
    columns = jnp.arange(span, dtype=jnp.int32)
    target = (columns[None, :] + block_shift[:, None]) % span
    moving = (target[:, :, None] == columns[None, None, :]).astype(jnp.float32)
    shifted = jnp.einsum("bsj,bjl->bsl", picked, moving, precision=lax.Precision.HIGHEST)
    return shifted.astype(jnp.bfloat16)


def banded_matrix(along):
    count = along.shape[0]
    identity = jnp.eye(count, dtype=jnp.bfloat16)
    return (along[:, :, None, :] * identity[:, None, :, None]).reshape(
        count * SLICES, count * BLOCK
    )


def halve(values, axis, me):
    half = values.shape[0] // 2
    keep = lax.dynamic_slice_in_dim(values, me * half, half, 0)
    give = lax.dynamic_slice_in_dim(values, (1 - me) * half, half, 0)
    got = lax.ppermute(give.astype(jnp.bfloat16), axis, [(0, 1), (1, 0)])
    return keep + got.astype(jnp.float32)


def double(values, axis, me):
    other = lax.ppermute(values, axis, [(0, 1), (1, 0)])
    low = jnp.where(me == 0, values, other)
    high = jnp.where(me == 0, other, values)
    return jnp.concatenate([low, high], 0)


def shards(volume, slices_x, slices_y, slices_z, profiles, profile_index, block_shift):
    planes, rows_here, width = volume.shape
    count_x = width // BLOCK
    count_y = slices_y.shape[1] // SLICES
    mats = block_mats(profiles, profile_index, block_shift)
    along_x = mats[:count_x]
    along_y = mats[count_x : count_x + count_y]
    along_z = mats[count_x + count_y :]
    coarse = volume.astype(jnp.bfloat16)

    banded_x = banded_matrix(along_x)
    flat_coarse = coarse.reshape(planes * rows_here, width)
    fwd_x = lax.dot_general(
        flat_coarse, banded_x, (((1,), (1,)), ((), ())), preferred_element_type=jnp.float32
    )
    resid_x = (
        slices_x.reshape(planes * rows_here, count_x * SLICES).astype(jnp.float32) - fwd_x
    ).astype(jnp.bfloat16)
    corr_x = jnp.dot(resid_x, banded_x, preferred_element_type=jnp.float32).reshape(
        planes, rows_here, width
    )

    zl = lax.axis_index("zl")
    co = lax.axis_index("co")
    rep = zl * 2 + co
    band_y = lax.dynamic_slice_in_dim(along_y[0], rep * rows_here, rows_here, 1)
    half = planes // 2
    keep_y = jnp.einsum(
        "sl,zlx->zsx",
        band_y,
        lax.dynamic_slice_in_dim(coarse, co * half, half, 0),
        preferred_element_type=jnp.float32,
    )
    give_y = jnp.einsum(
        "sl,zlx->zsx",
        band_y,
        lax.dynamic_slice_in_dim(coarse, (1 - co) * half, half, 0),
        preferred_element_type=jnp.float32,
    ).astype(jnp.bfloat16)
    fwd_y = keep_y + lax.ppermute(give_y, "co", [(0, 1), (1, 0)]).astype(jnp.float32)
    fwd_y = halve(fwd_y, "zl", zl)
    part_z = planes // 4
    obs_y = lax.dynamic_slice_in_dim(slices_y, (co * 2 + zl) * part_z, part_z, 0)
    resid_y = (obs_y.astype(jnp.float32) - fwd_y).astype(jnp.bfloat16)
    resid_y = double(resid_y, "zl", zl)
    resid_y = double(resid_y, "co", co)
    corr_y = jnp.einsum("sl,zsx->zlx", band_y, resid_y, preferred_element_type=jnp.float32)

    zb = lax.axis_index("zb")
    zq = lax.axis_index("zq")
    group = lax.axis_size("zq")
    mat_z = lax.dynamic_index_in_dim(along_z, zb, 0, keepdims=False)
    band_z = lax.dynamic_slice_in_dim(mat_z, zq * planes, planes, 1)
    piece = SLICES // group
    sheet = coarse.reshape(planes, rows_here * width)
    own_rows = lax.dynamic_slice_in_dim(band_z, zq * piece, piece, 0)
    fwd_z = jnp.dot(own_rows, sheet, preferred_element_type=jnp.float32)
    far_rows = jnp.stack(
        [lax.dynamic_slice_in_dim(band_z, ((zq + k) % group) * piece, piece, 0) for k in range(1, group)],
        0,
    )
    far_z = jnp.einsum(
        "ksl,lp->ksp", far_rows, sheet, preferred_element_type=jnp.float32
    ).astype(jnp.bfloat16)
    for k in range(1, group):
        sent = far_z[k - 1]
        got = lax.ppermute(sent, "zq", [(j, (j + k) % group) for j in range(group)])
        fwd_z = fwd_z + got.astype(jnp.float32)
    observed = slices_z.reshape(piece, rows_here * width).astype(jnp.float32)
    resid_z = (observed - fwd_z).astype(jnp.bfloat16)
    pieces = [resid_z]
    rows = [own_rows]
    for k in range(1, group):
        pieces.append(lax.ppermute(resid_z, "zq", [(j, (j + k) % group) for j in range(group)]))
        src = (zq - k + group) % group
        rows.append(lax.dynamic_slice_in_dim(band_z, src * piece, piece, 0))
    corr_z = lax.dot_general(
        jnp.concatenate(rows, 0),
        jnp.concatenate(pieces, 0),
        (((0,), (0,)), ((), ())),
        preferred_element_type=jnp.float32,
    ).reshape(planes, rows_here, width)

    return volume + step_size * (corr_x + corr_y + corr_z)


def solution(mesh):
    nslab, nrep = mesh.devices.shape
    slab = ("zb", "zq")
    rep = ("zl", "co")

    def run(volume, *rest):
        group = BLOCK // (volume.shape[0] // nslab)
        inner = Mesh(
            mesh.devices.reshape(nslab // group, group, 2, nrep // 2), ("zb", "zq", "zl", "co")
        )
        return jax.shard_map(
            shards,
            mesh=inner,
            in_specs=(
                P(slab, rep, None),
                P(slab, rep, None),
                P(slab, None, None),
                P(slab, rep, None),
                P(),
                P(),
                P(),
            ),
            out_specs=P(slab, rep, None),
            check_vma=False,
        )(volume, *rest)

    return run
```

```python
import jax
import jax.numpy as jnp
from jax import lax
from jax.sharding import Mesh, PartitionSpec as P

BLOCK = 128
SLICES = 16


step_size = 0.5


def block_mats(profiles, profile_index, block_shift):
    kinds = profiles.shape[0]
    span = profiles.shape[2]
    onehot = (profile_index[:, None] == jnp.arange(kinds, dtype=jnp.int32)[None, :]).astype(
        jnp.float32
    )
    picked = jnp.einsum("bk,ksl->bsl", onehot, profiles, precision=lax.Precision.HIGHEST)
    columns = jnp.arange(span, dtype=jnp.int32)
    target = (columns[None, :] + block_shift[:, None]) % span
    moving = (target[:, :, None] == columns[None, None, :]).astype(jnp.float32)
    shifted = jnp.einsum("bsj,bjl->bsl", picked, moving, precision=lax.Precision.HIGHEST)
    return shifted.astype(jnp.bfloat16)


def banded_matrix(along):
    count = along.shape[0]
    identity = jnp.eye(count, dtype=jnp.bfloat16)
    return (along[:, :, None, :] * identity[:, None, :, None]).reshape(
        count * SLICES, count * BLOCK
    )


def halve(values, axis, me):
    half = values.shape[0] // 2
    keep = lax.dynamic_slice_in_dim(values, me * half, half, 0)
    give = lax.dynamic_slice_in_dim(values, (1 - me) * half, half, 0)
    got = lax.ppermute(give.astype(jnp.bfloat16), axis, [(0, 1), (1, 0)])
    return keep + got.astype(jnp.float32)


def double(values, axis, me):
    other = lax.ppermute(values, axis, [(0, 1), (1, 0)])
    low = jnp.where(me == 0, values, other)
    high = jnp.where(me == 0, other, values)
    return jnp.concatenate([low, high], 0)


def shards(volume, slices_x, slices_y, slices_z, profiles, profile_index, block_shift):
    planes, rows_here, width = volume.shape
    count_x = width // BLOCK
    count_y = slices_y.shape[1] // SLICES
    mats = block_mats(profiles, profile_index, block_shift)
    along_x = mats[:count_x]
    along_y = mats[count_x : count_x + count_y]
    along_z = mats[count_x + count_y :]
    coarse = volume.astype(jnp.bfloat16)

    banded_x = banded_matrix(along_x)
    flat_coarse = coarse.reshape(planes * rows_here, width)
    fwd_x = lax.dot_general(
        flat_coarse, banded_x, (((1,), (1,)), ((), ())), preferred_element_type=jnp.float32
    )
    resid_x = (
        slices_x.reshape(planes * rows_here, count_x * SLICES).astype(jnp.float32) - fwd_x
    ).astype(jnp.bfloat16)
    corr_x = jnp.dot(resid_x, banded_x, preferred_element_type=jnp.float32).reshape(
        planes, rows_here, width
    )

    zl = lax.axis_index("zl")
    co = lax.axis_index("co")
    rep = zl * 2 + co
    band_y = lax.dynamic_slice_in_dim(along_y[0], rep * rows_here, rows_here, 1)
    half = planes // 2
    keep_y = jnp.einsum(
        "sl,zlx->zsx",
        band_y,
        lax.dynamic_slice_in_dim(coarse, co * half, half, 0),
        preferred_element_type=jnp.float32,
    )
    give_y = jnp.einsum(
        "sl,zlx->zsx",
        band_y,
        lax.dynamic_slice_in_dim(coarse, (1 - co) * half, half, 0),
        preferred_element_type=jnp.float32,
    ).astype(jnp.bfloat16)
    fwd_y = keep_y + lax.ppermute(give_y, "co", [(0, 1), (1, 0)]).astype(jnp.float32)
    fwd_y = halve(fwd_y, "zl", zl)
    part_z = planes // 4
    obs_y = lax.dynamic_slice_in_dim(slices_y, (co * 2 + zl) * part_z, part_z, 0)
    resid_y = (obs_y.astype(jnp.float32) - fwd_y).astype(jnp.bfloat16)
    resid_y = double(resid_y, "zl", zl)
    resid_y = double(resid_y, "co", co)
    corr_y = jnp.einsum("sl,zsx->zlx", band_y, resid_y, preferred_element_type=jnp.float32)

    zb = lax.axis_index("zb")
    zq = lax.axis_index("zq")
    group = lax.axis_size("zq")
    mat_z = lax.dynamic_index_in_dim(along_z, zb, 0, keepdims=False)
    band_z = lax.dynamic_slice_in_dim(mat_z, zq * planes, planes, 1)
    piece = SLICES // group
    sheet = coarse.reshape(planes, rows_here * width)
    own_rows = lax.dynamic_slice_in_dim(band_z, zq * piece, piece, 0)
    fwd_z = jnp.dot(own_rows, sheet, preferred_element_type=jnp.float32)
    far_rows = jnp.concatenate(
        [lax.dynamic_slice_in_dim(band_z, ((zq + k) % group) * piece, piece, 0) for k in range(1, group)],
        0,
    )
    far_z = jnp.dot(far_rows, sheet, preferred_element_type=jnp.float32).astype(jnp.bfloat16)
    for k in sorted(range(1, group), key=lambda k: -min(k, group - k)):
        sent = far_z[(k - 1) * piece : k * piece]
        got = lax.ppermute(sent, "zq", [(j, (j + k) % group) for j in range(group)])
        fwd_z = fwd_z + got.astype(jnp.float32)
    observed = slices_z.reshape(piece, rows_here * width).astype(jnp.float32)
    resid_z = (observed - fwd_z).astype(jnp.bfloat16)
    pieces = [resid_z]
    rows = [own_rows]
    for k in sorted(range(1, group), key=lambda k: -min(k, group - k)):
        pieces.append(lax.ppermute(resid_z, "zq", [(j, (j + k) % group) for j in range(group)]))
        src = (zq - k + group) % group
        rows.append(lax.dynamic_slice_in_dim(band_z, src * piece, piece, 0))
    corr_z = lax.dot_general(
        jnp.concatenate(rows, 0),
        jnp.concatenate(pieces, 0),
        (((0,), (0,)), ((), ())),
        preferred_element_type=jnp.float32,
    ).reshape(planes, rows_here, width)

    return volume + step_size * (corr_x + corr_y + corr_z)


def solution(mesh):
    nslab, nrep = mesh.devices.shape
    slab = ("zb", "zq")
    rep = ("zl", "co")

    def run(volume, *rest):
        group = BLOCK // (volume.shape[0] // nslab)
        inner = Mesh(
            mesh.devices.reshape(nslab // group, group, 2, nrep // 2), ("zb", "zq", "zl", "co")
        )
        return jax.shard_map(
            shards,
            mesh=inner,
            in_specs=(
                P(slab, rep, None),
                P(slab, rep, None),
                P(slab, None, None),
                P(slab, rep, None),
                P(),
                P(),
                P(),
            ),
            out_specs=P(slab, rep, None),
            check_vma=False,
        )(volume, *rest)

    return run
```

```python
import jax
import jax.numpy as jnp
from jax import lax
from jax.sharding import Mesh, PartitionSpec as P

BLOCK = 128
SLICES = 16


step_size = 0.5


def block_mats(profiles, profile_index, block_shift):
    kinds = profiles.shape[0]
    span = profiles.shape[2]
    onehot = (profile_index[:, None] == jnp.arange(kinds, dtype=jnp.int32)[None, :]).astype(
        jnp.float32
    )
    picked = jnp.einsum("bk,ksl->bsl", onehot, profiles, precision=lax.Precision.HIGHEST)
    columns = jnp.arange(span, dtype=jnp.int32)
    target = (columns[None, :] + block_shift[:, None]) % span
    moving = (target[:, :, None] == columns[None, None, :]).astype(jnp.float32)
    shifted = jnp.einsum("bsj,bjl->bsl", picked, moving, precision=lax.Precision.HIGHEST)
    return shifted.astype(jnp.bfloat16)


def banded_matrix(along):
    count = along.shape[0]
    identity = jnp.eye(count, dtype=jnp.bfloat16)
    return (along[:, :, None, :] * identity[:, None, :, None]).reshape(
        count * SLICES, count * BLOCK
    )


def halve(values, axis, me):
    half = values.shape[0] // 2
    keep = lax.dynamic_slice_in_dim(values, me * half, half, 0)
    give = lax.dynamic_slice_in_dim(values, (1 - me) * half, half, 0)
    got = lax.ppermute(give.astype(jnp.bfloat16), axis, [(0, 1), (1, 0)])
    return keep + got.astype(jnp.float32)


def double(values, axis, me):
    other = lax.ppermute(values, axis, [(0, 1), (1, 0)])
    low = jnp.where(me == 0, values, other)
    high = jnp.where(me == 0, other, values)
    return jnp.concatenate([low, high], 0)


def shards(volume, slices_x, slices_y, slices_z, profiles, profile_index, block_shift):
    planes, rows_here, width = volume.shape
    count_x = width // BLOCK
    count_y = slices_y.shape[1] // SLICES
    mats = block_mats(profiles, profile_index, block_shift)
    along_x = mats[:count_x]
    along_y = mats[count_x : count_x + count_y]
    along_z = mats[count_x + count_y :]
    coarse = volume.astype(jnp.bfloat16)

    banded_x = banded_matrix(along_x)
    flat_coarse = coarse.reshape(planes * rows_here, width)
    fwd_x = lax.dot_general(
        flat_coarse, banded_x, (((1,), (1,)), ((), ())), preferred_element_type=jnp.float32
    )
    resid_x = (
        slices_x.reshape(planes * rows_here, count_x * SLICES).astype(jnp.float32) - fwd_x
    ).astype(jnp.bfloat16)
    corr_x = jnp.dot(resid_x, banded_x, preferred_element_type=jnp.float32).reshape(
        planes, rows_here, width
    )

    zl = lax.axis_index("zl")
    co = lax.axis_index("co")
    rep = zl * 2 + co
    band_y = lax.dynamic_slice_in_dim(along_y[0], rep * rows_here, rows_here, 1)
    half = planes // 2
    keep_y = jnp.einsum(
        "sl,zlx->zsx",
        band_y,
        lax.dynamic_slice_in_dim(coarse, co * half, half, 0),
        preferred_element_type=jnp.float32,
    )
    give_y = jnp.einsum(
        "sl,zlx->zsx",
        band_y,
        lax.dynamic_slice_in_dim(coarse, (1 - co) * half, half, 0),
        preferred_element_type=jnp.float32,
    ).astype(jnp.bfloat16)
    fwd_y = keep_y + lax.ppermute(give_y, "co", [(0, 1), (1, 0)]).astype(jnp.float32)
    fwd_y = halve(fwd_y, "zl", zl)
    part_z = planes // 4
    obs_y = lax.dynamic_slice_in_dim(slices_y, (co * 2 + zl) * part_z, part_z, 0)
    resid_y = (obs_y.astype(jnp.float32) - fwd_y).astype(jnp.bfloat16)
    resid_y = double(resid_y, "zl", zl)
    resid_y = double(resid_y, "co", co)
    corr_y = jnp.einsum("sl,zsx->zlx", band_y, resid_y, preferred_element_type=jnp.float32)

    zb = lax.axis_index("zb")
    zq = lax.axis_index("zq")
    group = lax.axis_size("zq")
    mat_z = lax.dynamic_index_in_dim(along_z, zb, 0, keepdims=False)
    band_z = lax.dynamic_slice_in_dim(mat_z, zq * planes, planes, 1)
    piece = SLICES // group
    sheet = coarse.reshape(planes, rows_here * width)
    own_rows = lax.dynamic_slice_in_dim(band_z, zq * piece, piece, 0)
    fwd_z = jnp.dot(own_rows, sheet, preferred_element_type=jnp.float32)
    far_rows = jnp.concatenate(
        [lax.dynamic_slice_in_dim(band_z, ((zq + k) % group) * piece, piece, 0) for k in range(1, group)],
        0,
    )
    far_z = jnp.dot(far_rows, sheet, preferred_element_type=jnp.float32).astype(jnp.bfloat16)
    for k in range(1, group):
        sent = far_z[(k - 1) * piece : k * piece]
        got = lax.ppermute(sent, "zq", [(j, (j + k) % group) for j in range(group)])
        fwd_z = fwd_z + got.astype(jnp.float32)
    observed = slices_z.reshape(piece, rows_here * width).astype(jnp.float32)
    resid_z = (observed - fwd_z).astype(jnp.bfloat16)
    pieces = [resid_z]
    rows = [own_rows]
    for k in range(1, group):
        pieces.append(lax.ppermute(resid_z, "zq", [(j, (j + k) % group) for j in range(group)]))
        src = (zq - k + group) % group
        rows.append(lax.dynamic_slice_in_dim(band_z, src * piece, piece, 0))
    corr_z = lax.dot_general(
        jnp.concatenate(rows, 0),
        jnp.concatenate(pieces, 0),
        (((0,), (0,)), ((), ())),
        preferred_element_type=jnp.float32,
    ).reshape(planes, rows_here, width)

    base = lax.optimization_barrier(volume + step_size * corr_x)
    return base + step_size * (corr_y + corr_z)


def solution(mesh):
    nslab, nrep = mesh.devices.shape
    slab = ("zb", "zq")
    rep = ("zl", "co")

    def run(volume, *rest):
        group = BLOCK // (volume.shape[0] // nslab)
        inner = Mesh(
            mesh.devices.reshape(nslab // group, group, 2, nrep // 2), ("zb", "zq", "zl", "co")
        )
        return jax.shard_map(
            shards,
            mesh=inner,
            in_specs=(
                P(slab, rep, None),
                P(slab, rep, None),
                P(slab, None, None),
                P(slab, rep, None),
                P(),
                P(),
                P(),
            ),
            out_specs=P(slab, rep, None),
            check_vma=False,
        )(volume, *rest)

    return run
```

```python
import jax
import jax.numpy as jnp
from jax import lax
from jax.sharding import Mesh, PartitionSpec as P

BLOCK = 128
SLICES = 16


step_size = 0.5


def block_mats(profiles, profile_index, block_shift):
    kinds = profiles.shape[0]
    span = profiles.shape[2]
    onehot = (profile_index[:, None] == jnp.arange(kinds, dtype=jnp.int32)[None, :]).astype(
        jnp.float32
    )
    picked = jnp.einsum("bk,ksl->bsl", onehot, profiles, precision=lax.Precision.HIGHEST)
    columns = jnp.arange(span, dtype=jnp.int32)
    target = (columns[None, :] + block_shift[:, None]) % span
    moving = (target[:, :, None] == columns[None, None, :]).astype(jnp.float32)
    shifted = jnp.einsum("bsj,bjl->bsl", picked, moving, precision=lax.Precision.HIGHEST)
    return shifted.astype(jnp.bfloat16)


def banded_matrix(along):
    count = along.shape[0]
    identity = jnp.eye(count, dtype=jnp.bfloat16)
    return (along[:, :, None, :] * identity[:, None, :, None]).reshape(
        count * SLICES, count * BLOCK
    )


def halve(values, axis, me):
    half = values.shape[0] // 2
    keep = lax.dynamic_slice_in_dim(values, me * half, half, 0)
    give = lax.dynamic_slice_in_dim(values, (1 - me) * half, half, 0)
    got = lax.ppermute(give.astype(jnp.bfloat16), axis, [(0, 1), (1, 0)])
    return keep + got.astype(jnp.float32)


def double(values, axis, me):
    other = lax.ppermute(values, axis, [(0, 1), (1, 0)])
    low = jnp.where(me == 0, values, other)
    high = jnp.where(me == 0, other, values)
    return jnp.concatenate([low, high], 0)


def shards(volume, slices_x, slices_y, slices_z, profiles, profile_index, block_shift):
    planes, rows_here, width = volume.shape
    count_x = width // BLOCK
    count_y = slices_y.shape[1] // SLICES
    mats = block_mats(profiles, profile_index, block_shift)
    along_x = mats[:count_x]
    along_y = mats[count_x : count_x + count_y]
    along_z = mats[count_x + count_y :]
    coarse = volume.astype(jnp.bfloat16)

    banded_x = banded_matrix(along_x)
    flat_coarse = coarse.reshape(planes * rows_here, width)
    fwd_x = lax.dot_general(
        flat_coarse, banded_x, (((1,), (1,)), ((), ())), preferred_element_type=jnp.float32
    )
    resid_x = (
        slices_x.reshape(planes * rows_here, count_x * SLICES).astype(jnp.float32) - fwd_x
    ).astype(jnp.bfloat16)
    corr_x = jnp.dot(resid_x, banded_x, preferred_element_type=jnp.float32).reshape(
        planes, rows_here, width
    )

    zl = lax.axis_index("zl")
    co = lax.axis_index("co")
    rep = zl * 2 + co
    band_y = lax.dynamic_slice_in_dim(along_y[0], rep * rows_here, rows_here, 1)
    half = planes // 2
    keep_y = jnp.einsum(
        "sl,zlx->zsx",
        band_y,
        lax.dynamic_slice_in_dim(coarse, co * half, half, 0),
        preferred_element_type=jnp.float32,
    )
    give_y = jnp.einsum(
        "sl,zlx->zsx",
        band_y,
        lax.dynamic_slice_in_dim(coarse, (1 - co) * half, half, 0),
        preferred_element_type=jnp.float32,
    ).astype(jnp.bfloat16)
    fwd_y = keep_y + lax.ppermute(give_y, "co", [(0, 1), (1, 0)]).astype(jnp.float32)
    fwd_y = halve(fwd_y, "zl", zl)
    part_z = planes // 4
    obs_y = lax.dynamic_slice_in_dim(slices_y, (co * 2 + zl) * part_z, part_z, 0)
    resid_y = (obs_y.astype(jnp.float32) - fwd_y).astype(jnp.bfloat16)
    resid_y = double(resid_y, "zl", zl)
    resid_y = double(resid_y, "co", co)
    corr_y = jnp.einsum("sl,zsx->zlx", band_y, resid_y, preferred_element_type=jnp.float32)

    zb = lax.axis_index("zb")
    zq = lax.axis_index("zq")
    group = lax.axis_size("zq")
    mat_z = lax.dynamic_index_in_dim(along_z, zb, 0, keepdims=False)
    band_z = lax.dynamic_slice_in_dim(mat_z, zq * planes, planes, 1)
    piece = SLICES // group
    sheet = coarse.reshape(planes, rows_here * width)
    own_rows = lax.dynamic_slice_in_dim(band_z, zq * piece, piece, 0)
    fwd_z = jnp.dot(own_rows, sheet, preferred_element_type=jnp.float32)
    far_rows = jnp.concatenate(
        [lax.dynamic_slice_in_dim(band_z, ((zq + k) % group) * piece, piece, 0) for k in range(1, group)],
        0,
    )
    far_z = jnp.dot(far_rows, sheet, preferred_element_type=jnp.float32).astype(jnp.bfloat16)
    for k in sorted(range(1, group), key=lambda k: -min(k, group - k)):
        sent = far_z[(k - 1) * piece : k * piece]
        got = lax.ppermute(sent, "zq", [(j, (j + k) % group) for j in range(group)])
        fwd_z = fwd_z + got.astype(jnp.float32)
    observed = slices_z.reshape(piece, rows_here * width).astype(jnp.float32)
    resid_z = (observed - fwd_z).astype(jnp.bfloat16)
    pieces = [resid_z]
    rows = [own_rows]
    for k in sorted(range(1, group), key=lambda k: -min(k, group - k)):
        pieces.append(lax.ppermute(resid_z, "zq", [(j, (j + k) % group) for j in range(group)]))
        src = (zq - k + group) % group
        rows.append(lax.dynamic_slice_in_dim(band_z, src * piece, piece, 0))
    corr_z = lax.dot_general(
        jnp.concatenate(rows, 0),
        jnp.concatenate(pieces, 0),
        (((0,), (0,)), ((), ())),
        preferred_element_type=jnp.float32,
    ).reshape(planes, rows_here, width)

    base = lax.optimization_barrier(volume + step_size * corr_x)
    return base + step_size * (corr_y + corr_z)


def solution(mesh):
    nslab, nrep = mesh.devices.shape
    slab = ("zb", "zq")
    rep = ("zl", "co")

    def run(volume, *rest):
        group = BLOCK // (volume.shape[0] // nslab)
        inner = Mesh(
            mesh.devices.reshape(nslab // group, group, 2, nrep // 2), ("zb", "zq", "zl", "co")
        )
        return jax.shard_map(
            shards,
            mesh=inner,
            in_specs=(
                P(slab, rep, None),
                P(slab, rep, None),
                P(slab, None, None),
                P(slab, rep, None),
                P(),
                P(),
                P(),
            ),
            out_specs=P(slab, rep, None),
            check_vma=False,
        )(volume, *rest)

    return run
```
